256 devices in a mesh: section: 16 (over y_lo, x, core), expert: 16 (over z, y_hi).
Axes of the slice: x: 4, y: 4 (y_hi: 2, y_lo: 2; y = y_hi * 2 + y_lo), z: 8, core: 2. Of those that a mesh axis runs over, the one named last changes fastest.
Arguments:
- activations: bfloat16 [16384, 8192], P('section', 'expert'), may hold values from -12 to 12
- modality: int32 [16384], P('section'), may hold values from 0 to 1
- selected: int32 [16, 256], P('section'), may hold values from 0 to 1023, as said below
- routes: int32 [4096, 1], P('section'), may hold values from 0 to 15, as said below
- norm_gain: float32 [2, 8192], P(None, 'expert'), may hold values from 0.1 to 1.9
- router: float32 [8192], P('expert'), may hold values from -0.0625 to 0.0625
- gate_w: bfloat16 [16, 3072, 8192], P('expert', 'section'), may hold values from -0.0625 to 0.0625
- up_w: bfloat16 [16, 3072, 8192], P('expert', 'section'), may hold values from -0.0625 to 0.0625
- down_w: bfloat16 [16, 3072, 8192], P('expert', 'section'), may hold values from -0.21875 to 0.21875
Outputs:
- block_out: bfloat16 [16384, 8192], P('section', 'expert')
The draws below stay inside these ranges and needn't reach their ends.
Inputs may be any that keep to these rules, and one draw needn't show every extreme that they name: Each row of selected lists 256 different positions in rising order, the first and the last position among them. `routes`: among the 256 rows of one section group no expert is named more than 24 times, and some expert exactly 24 times; the entry for selected[s, j] is below 8 if that token's modality is 0, and 8 or more if it is 1.
All inputs are finite; a program needn't handle non-finite values.
Results may differ from the reference program's by a relative error of at most 0.0075.
Values may be sent and summed in bfloat16 or wider, within the bound.
No kernel may reach another device: no remote copies, remote signals or barrier semaphores. Data moves between devices by JAX's collectives and lax.ppermute only.
A program may use at most 128 MiB of HBM per device.

```python
import math
import jax
import jax.numpy as jnp
from jax import lax

D = 8192
FF = 3072
TOK_SECTION = 1024
EXPERTS = 16
SEL_SECTION = 256
CAP = 24
HID_DEV = 192
TOKENS = 16384
N_SECTION = 16


def draw_activations(key, part):
    first, second = jax.random.split(key)
    base = jax.random.normal(first, (TOKENS, D), jnp.float32)
    columns = jnp.arange(D, dtype=jnp.float32) / D
    col_scale = 3.0 ** (columns - 0.5)
    row_scale = jnp.exp(jax.random.uniform(second, (TOKENS, 1), jnp.float32, math.log(0.6), math.log(1.6)))
    return jnp.clip(base * col_scale[None, :] * row_scale, -12.0, 12.0).astype(jnp.bfloat16)


def section_block(block_key):
    sel_key, bias_key, force_key, noise_key, mix_key, kind_key = jax.random.split(block_key, 6)
    order = jax.random.permutation(sel_key, TOK_SECTION).astype(jnp.int32)
    places = jnp.arange(TOK_SECTION, dtype=jnp.int32)
    order = jnp.where(places == 0, -2, order)
    order = jnp.where(places == TOK_SECTION - 1, -1, order)
    chosen = jnp.sort(jnp.argsort(order, stable=True)[:SEL_SECTION].astype(jnp.int32))
    slot_total = EXPERTS * CAP
    bias = jax.random.randint(bias_key, (EXPERTS,), 0, 4).astype(jnp.int32)
    forced = jax.random.randint(force_key, (), 0, EXPERTS).astype(jnp.int32)
    bias = jnp.where(jnp.arange(EXPERTS, dtype=jnp.int32) == forced, 8, bias)
    owners = jnp.arange(slot_total, dtype=jnp.int32) // CAP
    noise = jax.random.randint(noise_key, (slot_total,), 0, 65536).astype(jnp.int32)
    scores = (bias[owners] * 65536 + noise) * slot_total + jnp.arange(slot_total, dtype=jnp.int32)
    taken = jnp.argsort(-scores)[:SEL_SECTION].astype(jnp.int32)
    experts = owners[taken]
    experts = experts[jax.random.permutation(mix_key, SEL_SECTION)].astype(jnp.int32)
    kinds = jax.random.randint(kind_key, (TOK_SECTION,), 0, 2).astype(jnp.int32)
    kinds = kinds.at[chosen].set((experts >= EXPERTS // 2).astype(jnp.int32))
    return (chosen, experts, kinds)


def common_draw(key):
    base = jax.random.fold_in(key, 7321)
    keys = jax.vmap(lambda index: jax.random.fold_in(base, index))(jnp.arange(N_SECTION, dtype=jnp.int32))
    return jax.vmap(section_block)(keys)


def draw_selected(key, part):
    chosen, experts, kinds = common_draw(key)
    return chosen.astype(jnp.int32)


def draw_routes(key, part):
    chosen, experts, kinds = common_draw(key)
    return experts.reshape(N_SECTION * SEL_SECTION, 1).astype(jnp.int32)


def draw_modality(key, part):
    chosen, experts, kinds = common_draw(key)
    return kinds.reshape(TOKENS).astype(jnp.int32)


def level_of(rng, dims, cuts, smallest, top_value):
    factor_of, own = 1.0, jax.random.fold_in(rng, 6)
    for axis_at, blocks in cuts:
        draws = jnp.exp(jax.random.uniform(jax.random.fold_in(own, axis_at), (blocks,), jnp.float32, smallest / len(cuts), top_value / len(cuts)))
        factor_of = factor_of * jnp.repeat(draws, dims[axis_at] // blocks).reshape([-1 if axis == axis_at else 1 for axis in range(len(dims))])
    return factor_of


def normal_values(key, shape, scale, bound, cuts=(), kind=jnp.bfloat16):
    drawn = jax.random.normal(key, shape, jnp.float32) * scale
    if len(cuts) > 0:
        drawn = level_of(key, shape, cuts, -0.22, 0.18) * drawn
    return jnp.clip(drawn, min=-bound, max=bound).astype(kind)


def setup_inputs(seed: int = 0) -> dict:
    streams_of = jax.random.split(jax.random.key(seed), 10)
    return {
        "activations": draw_activations(jax.random.fold_in(streams_of[9], 71), 0),
        "modality": draw_modality(jax.random.fold_in(streams_of[9], 71), 0),
        "selected": draw_selected(jax.random.fold_in(streams_of[9], 71), 0),
        "routes": draw_routes(jax.random.fold_in(streams_of[9], 71), 0),
        "norm_gain": jnp.clip(1.0 + 0.18 * jax.random.normal(streams_of[4], (2, D), jnp.float32), 0.1, 1.9),
        "router": normal_values(streams_of[5], (D,), D ** -0.5, 0.0625, ((0, 16),), jnp.float32),
        "gate_w": normal_values(streams_of[6], (EXPERTS, FF, D), D ** -0.5, 0.0625, ((0, 16), (1, 16))),
        "up_w": normal_values(streams_of[7], (EXPERTS, FF, D), D ** -0.5, 0.0625, ((0, 16), (1, 16))),
        "down_w": normal_values(streams_of[8], (EXPERTS, FF, D), (FF // 4) ** -0.5, 0.21875, ((0, 16), (1, 16))),
    }


EPS = 1e-05

def reference(activations, modality, selected, routes, norm_gain, router, gate_w, up_w, down_w):
    arrived = jnp.roll(activations, TOK_SECTION, axis=0)
    offsets = (jnp.arange(N_SECTION, dtype=jnp.int32) * TOK_SECTION)[:, None]
    picks = (selected + offsets).reshape(-1).astype(jnp.int32)
    picked = arrived[picks].astype(jnp.float32)
    kinds = modality[picks]
    gains = jnp.where(kinds[:, None] == 1, norm_gain[1][None, :], norm_gain[0][None, :])
    scale = lax.rsqrt(lax.optimization_barrier(jnp.sum(picked * picked, axis=1)) / D + EPS)
    normed = (picked * scale[:, None] * gains).astype(jnp.bfloat16)
    score = jax.nn.sigmoid(scale * lax.optimization_barrier(jnp.sum(picked * gains * router[None, :], axis=1)))
    experts = routes[:, 0].reshape(N_SECTION, SEL_SECTION).astype(jnp.int32)
    onehot = (experts[:, :, None] == jnp.arange(EXPERTS, dtype=jnp.int32)[None, None, :]).astype(jnp.int32)
    ranks = jnp.cumsum(onehot, axis=1) - 1
    slot = lax.optimization_barrier(jnp.sum(ranks * onehot, axis=2)).astype(jnp.int32)
    position = (jnp.arange(N_SECTION, dtype=jnp.int32)[:, None] * CAP + slot).reshape(-1).astype(jnp.int32)
    flat_experts = experts.reshape(-1)
    buffers = jnp.zeros((EXPERTS, N_SECTION * CAP, D), jnp.bfloat16).at[flat_experts, position].set(normed)

    def one_expert(items):
        buffer, wgate, wup, wdown = items
        gate = jnp.dot(buffer, wgate.T, preferred_element_type=jnp.float32)
        upper = jnp.dot(buffer, wup.T, preferred_element_type=jnp.float32)
        hidden = (jax.nn.silu(gate) * upper).astype(jnp.bfloat16)
        blocks = hidden.astype(jnp.float32).reshape(N_SECTION * CAP, N_SECTION, HID_DEV)
        weights = wdown.astype(jnp.float32).reshape(N_SECTION, HID_DEV, D)
        parts = jnp.einsum('rbk,bkc->brc', blocks, weights)
        parts = lax.optimization_barrier(parts.astype(jnp.bfloat16)).astype(jnp.float32)
        return lax.optimization_barrier(jnp.sum(parts, axis=0)).astype(jnp.bfloat16)
    expert_out = lax.map(one_expert, (buffers, gate_w, up_w, down_w))
    rows_out = expert_out[flat_experts, position].astype(jnp.float32)
    result = arrived.astype(jnp.float32).at[picks].add(score[:, None] * rows_out)
    return result.astype(jnp.bfloat16)
```

```python
import jax
import jax.numpy as jnp
from jax import lax
from jax.sharding import PartitionSpec as P


EPS = 1e-05


def passed_along(block, axis, distance):
    devices = range(lax.axis_size(axis))
    route = [((i - distance) % len(devices), i) for i in devices]
    return lax.ppermute(block, axis, route)


def feature_product(block, weight):
    return lax.dot_general(
        block, weight, (((1,), (1,)), ((), ())), preferred_element_type=jnp.float32
    )


def slots_of(experts, expert_count):
    onehot = (experts[:, None] == jnp.arange(expert_count, dtype=jnp.int32)[None, :]).astype(
        jnp.int32
    )
    ranks = jnp.cumsum(onehot, axis=0) - 1
    return jnp.sum(ranks * onehot, axis=1)


def body(activations, modality, selected, routes, norm_gain, router, gate_w, up_w, down_w):
    n_section = lax.axis_size("section")
    sel_count = selected.shape[1]
    expert_count = lax.axis_size("expert") * gate_w.shape[0]
    capacity = max(2, 3 * sel_count // (2 * expert_count))
    groups = n_section

    arrived = passed_along(activations, "section", 1)

    sel_next = passed_along(selected, "section", -1)[0]
    routes_next = passed_along(routes, "section", -1)[:, 0]
    rows = activations[sel_next]
    target = routes_next * capacity + slots_of(routes_next, expert_count)
    placing = (
        target[None, :] == jnp.arange(expert_count * capacity, dtype=jnp.int32)[:, None]
    ).astype(jnp.bfloat16)
    feature_width = rows.shape[1]
    buffer = jnp.dot(placing, rows, preferred_element_type=jnp.float32).astype(jnp.bfloat16)
    buffer = buffer.reshape(expert_count, capacity, feature_width)
    mine = lax.all_to_all(buffer, "expert", split_axis=0, concat_axis=2, tiled=True)[0]

    n_exp_dev = lax.axis_size("expert")
    local_width = router.shape[0]
    tables = jnp.concatenate([norm_gain, router[None, :]], axis=0)
    tables = jnp.broadcast_to(tables[None], (n_exp_dev,) + tables.shape)
    tables = lax.all_to_all(tables, "expert", split_axis=0, concat_axis=0, tiled=True)
    tables = tables.transpose(1, 0, 2).reshape(tables.shape[1], n_exp_dev * local_width)
    gains_all = tables[:2]
    router_all = tables[2]
    expert_id = lax.axis_index("expert")
    kind = (expert_id >= expert_count // 2).astype(jnp.int32)
    gains = lax.dynamic_index_in_dim(gains_all, kind, axis=0, keepdims=False)
    picked = mine.astype(jnp.float32)
    d = picked.shape[1]
    scale = lax.rsqrt(jnp.sum(picked * picked, axis=1) / d + EPS)
    normed = (picked * scale[:, None] * gains[None, :]).astype(jnp.bfloat16)
    score = jax.nn.sigmoid(scale * jnp.sum(picked * gains[None, :] * router_all[None, :], axis=1))
    score_home = passed_along(score, "section", 1)

    block = lax.all_gather(normed, "section", axis=0, tiled=True)
    gate = feature_product(block, gate_w[0])
    upper = feature_product(block, up_w[0])
    hidden = (jax.nn.silu(gate) * upper).astype(jnp.bfloat16)
    hidden_width = hidden.shape[1]
    hidden = jnp.roll(hidden.reshape(groups, capacity, hidden_width), 1, axis=0).reshape(
        groups * capacity, hidden_width
    )
    part = jnp.dot(hidden, down_w[0], preferred_element_type=jnp.float32)
    summed = lax.psum_scatter(
        lax.optimization_barrier(part.astype(jnp.bfloat16))
        .astype(jnp.float32)
        .astype(jnp.bfloat16),
        "section",
        scatter_dimension=0,
        tiled=True,
    )
    update_rows = score_home[:, None] * summed.astype(jnp.float32)
    outgoing = update_rows.reshape(capacity, n_exp_dev, local_width).transpose(1, 0, 2)
    back = lax.all_to_all(outgoing, "expert", split_axis=0, concat_axis=0, tiled=True)
    flat_back = back.reshape(expert_count * capacity, local_width)

    picks = selected[0]
    experts = routes[:, 0]
    position = experts * capacity + slots_of(experts, expert_count)
    update = flat_back[position]
    result = arrived.astype(jnp.float32).at[picks].add(update)
    return result.astype(jnp.bfloat16)


def solution(mesh):
    placed = (
        P("section", "expert"),
        P("section"),
        P("section", None),
        P("section", None),
        P(None, "expert"),
        P("expert"),
        P("expert", "section", None),
        P("expert", "section", None),
        P("expert", "section", None),
    )
    return jax.shard_map(
        body, mesh=mesh, in_specs=placed, out_specs=P("section", "expert"), check_vma=False
    )
```

```python
import jax
import jax.numpy as jnp
from jax import lax
from jax.sharding import PartitionSpec as P


EPS = 1e-05


SECTION = ("chip", "core")


def passed_along(block, axis, distance):
    count = 1
    for name in axis:
        count *= lax.axis_size(name)
    route = [((i - distance) % count, i) for i in range(count)]
    return lax.ppermute(block, axis, route)


def feature_product(block, weight):
    return lax.dot_general(
        block, weight, (((1,), (1,)), ((), ())), preferred_element_type=jnp.float32
    )


def slots_of(experts, expert_count):
    onehot = (experts[:, None] == jnp.arange(expert_count, dtype=jnp.int32)[None, :]).astype(
        jnp.int32
    )
    ranks = jnp.cumsum(onehot, axis=0) - 1
    return jnp.sum(ranks * onehot, axis=1)


def body(activations, modality, selected, routes, norm_gain, router, gate_w, up_w, down_w):
    n_chip = lax.axis_size("chip")
    n_core = lax.axis_size("core")
    n_section = n_chip * n_core
    sel_count = selected.shape[1]
    expert_count = lax.axis_size("expert") * gate_w.shape[0]
    capacity = max(2, 3 * sel_count // (2 * expert_count))
    groups = n_section

    arrived = passed_along(activations, SECTION, 1)

    sel_next = passed_along(selected, SECTION, -1)[0]
    routes_next = passed_along(routes, SECTION, -1)[:, 0]
    rows = activations[sel_next]
    target = routes_next * capacity + slots_of(routes_next, expert_count)
    placing = (
        target[None, :] == jnp.arange(expert_count * capacity, dtype=jnp.int32)[:, None]
    ).astype(jnp.bfloat16)
    feature_width = rows.shape[1]
    buffer = jnp.dot(placing, rows, preferred_element_type=jnp.float32).astype(jnp.bfloat16)
    buffer = buffer.reshape(expert_count, capacity, feature_width)
    mine = lax.all_to_all(buffer, "expert", split_axis=0, concat_axis=2, tiled=True)[0]
    arrived, mine = lax.optimization_barrier((arrived, mine))

    n_exp_dev = lax.axis_size("expert")
    local_width = router.shape[0]
    tables = jnp.concatenate([norm_gain, router[None, :]], axis=0)
    tables = jnp.broadcast_to(tables[None], (n_exp_dev,) + tables.shape)
    tables = lax.all_to_all(tables, "expert", split_axis=0, concat_axis=0, tiled=True)
    tables = tables.transpose(1, 0, 2).reshape(tables.shape[1], n_exp_dev * local_width)
    gains_all = tables[:2]
    router_all = tables[2]
    expert_id = lax.axis_index("expert")
    kind = (expert_id >= expert_count // 2).astype(jnp.int32)
    gains = lax.dynamic_index_in_dim(gains_all, kind, axis=0, keepdims=False)
    picked = mine.astype(jnp.float32)
    d = picked.shape[1]
    scale = lax.rsqrt(jnp.sum(picked * picked, axis=1) / d + EPS)
    normed = (picked * scale[:, None] * gains[None, :]).astype(jnp.bfloat16)
    score = jax.nn.sigmoid(scale * jnp.sum(picked * gains[None, :] * router_all[None, :], axis=1))
    score_home = passed_along(score, SECTION, 1)

    block = lax.all_gather(normed, "chip", axis=0, tiled=True)
    block = lax.all_gather(block, "core", axis=0, tiled=True)
    gate = feature_product(block, gate_w[0])
    upper = feature_product(block, up_w[0])
    hidden = (jax.nn.silu(gate) * upper).astype(jnp.bfloat16)
    hidden_width = hidden.shape[1]
    order = []
    for core in range(n_core):
        for chip in range(n_chip):
            host = (chip * n_core + core - 1) % n_section
            order.append((host % n_core) * n_chip + host // n_core)
    hidden = jnp.take(
        hidden.reshape(groups, capacity, hidden_width), jnp.array(order, jnp.int32), axis=0
    ).reshape(groups * capacity, hidden_width)
    part = jnp.dot(hidden, down_w[0], preferred_element_type=jnp.float32)
    partial = (
        lax.optimization_barrier(part.astype(jnp.bfloat16)).astype(jnp.float32).astype(jnp.bfloat16)
    )
    summed = lax.psum_scatter(partial, "core", scatter_dimension=0, tiled=True)
    summed = lax.psum_scatter(summed, "chip", scatter_dimension=0, tiled=True)
    update_rows = score_home[:, None] * summed.astype(jnp.float32)
    outgoing = update_rows.reshape(capacity, n_exp_dev, local_width).transpose(1, 0, 2)
    back = lax.all_to_all(outgoing, "expert", split_axis=0, concat_axis=0, tiled=True)
    flat_back = back.reshape(expert_count * capacity, local_width)

    picks = selected[0]
    experts = routes[:, 0]
    position = experts * capacity + slots_of(experts, expert_count)
    update = flat_back[position]
    result = arrived.astype(jnp.float32).at[picks].add(update)
    return result.astype(jnp.bfloat16)


def solution(mesh):
    n_section, n_expert = mesh.devices.shape
    split = jax.sharding.Mesh(
        mesh.devices.reshape(n_section // 2, 2, n_expert), ("chip", "core", "expert")
    )
    placed = (
        P(SECTION, "expert"),
        P(SECTION),
        P(SECTION, None),
        P(SECTION, None),
        P(None, "expert"),
        P("expert"),
        P("expert", SECTION, None),
        P("expert", SECTION, None),
        P("expert", SECTION, None),
    )
    return jax.shard_map(
        body, mesh=split, in_specs=placed, out_specs=P(SECTION, "expert"), check_vma=False
    )
```

```python
import jax
import jax.numpy as jnp
from jax import lax
from jax.sharding import PartitionSpec as P


EPS = 1e-05


def passed_along(block, axis, distance):
    devices = range(lax.axis_size(axis))
    route = [((i - distance) % len(devices), i) for i in devices]
    return lax.ppermute(block, axis, route)


def feature_product(block, weight):
    return lax.dot_general(
        block, weight, (((1,), (1,)), ((), ())), preferred_element_type=jnp.float32
    )


def slots_of(experts, expert_count):
    onehot = (experts[:, None] == jnp.arange(expert_count, dtype=jnp.int32)[None, :]).astype(
        jnp.int32
    )
    ranks = jnp.cumsum(onehot, axis=0) - 1
    return jnp.sum(ranks * onehot, axis=1)


def body(activations, modality, selected, routes, norm_gain, router, gate_w, up_w, down_w):
    n_section = lax.axis_size("section")
    sel_count = selected.shape[1]
    expert_count = lax.axis_size("expert") * gate_w.shape[0]
    capacity = max(2, 3 * sel_count // (2 * expert_count))
    groups = n_section

    arrived = passed_along(activations, "section", 1)

    sel_next = passed_along(selected, "section", -1)[0]
    routes_next = passed_along(routes, "section", -1)[:, 0]
    rows = activations[sel_next]
    target = routes_next * capacity + slots_of(routes_next, expert_count)
    placing = (
        target[None, :] == jnp.arange(expert_count * capacity, dtype=jnp.int32)[:, None]
    ).astype(jnp.bfloat16)
    feature_width = rows.shape[1]
    buffer = jnp.dot(placing, rows, preferred_element_type=jnp.float32).astype(jnp.bfloat16)
    buffer = buffer.reshape(expert_count, capacity, feature_width)
    n_exp_dev = lax.axis_size("expert")
    local_width = router.shape[0]
    tables = jnp.concatenate([norm_gain, router[None, :]], axis=0)
    parts = []
    rest = tables
    for _ in range(3):
        piece = rest.astype(jnp.bfloat16)
        parts.append(piece)
        rest = rest - piece.astype(jnp.float32)
    table_rows = tables.shape[0]
    extra = jnp.broadcast_to(
        jnp.concatenate(parts, axis=0)[None], (expert_count, 3 * table_rows, local_width)
    )
    buffer = jnp.concatenate([buffer, extra], axis=1)
    mine = lax.all_to_all(buffer, "expert", split_axis=0, concat_axis=2, tiled=True)[0]
    arrived, mine = lax.optimization_barrier((arrived, mine))
    coded = mine[capacity:].astype(jnp.float32).reshape(3, table_rows, mine.shape[1])
    tables = (coded[0] + coded[1]) + coded[2]
    mine = mine[:capacity]

    gains_all = tables[:2]
    router_all = tables[2]
    expert_id = lax.axis_index("expert")
    kind = (expert_id >= expert_count // 2).astype(jnp.int32)
    gains = lax.dynamic_index_in_dim(gains_all, kind, axis=0, keepdims=False)
    picked = mine.astype(jnp.float32)
    d = picked.shape[1]
    scale = lax.rsqrt(jnp.sum(picked * picked, axis=1) / d + EPS)
    normed = (picked * scale[:, None] * gains[None, :]).astype(jnp.bfloat16)
    score = jax.nn.sigmoid(scale * jnp.sum(picked * gains[None, :] * router_all[None, :], axis=1))
    score_home = passed_along(score, "section", 1)

    block = lax.all_gather(normed, "section", axis=0, tiled=True)
    block, score_home = lax.optimization_barrier((block, score_home))
    gate = feature_product(block, gate_w[0])
    upper = feature_product(block, up_w[0])
    hidden = (jax.nn.silu(gate) * upper).astype(jnp.bfloat16)
    hidden_width = hidden.shape[1]
    hidden = jnp.roll(hidden.reshape(groups, capacity, hidden_width), 1, axis=0).reshape(
        groups * capacity, hidden_width
    )
    part = jnp.dot(hidden, down_w[0], preferred_element_type=jnp.float32)
    summed = lax.psum_scatter(
        lax.optimization_barrier(part.astype(jnp.bfloat16))
        .astype(jnp.float32)
        .astype(jnp.bfloat16),
        "section",
        scatter_dimension=0,
        tiled=True,
    )
    update_rows = (score_home[:, None] * summed.astype(jnp.float32)).astype(jnp.bfloat16)
    outgoing = update_rows.reshape(capacity, n_exp_dev, local_width).transpose(1, 0, 2)
    back = lax.all_to_all(outgoing, "expert", split_axis=0, concat_axis=0, tiled=True)
    flat_back = back.reshape(expert_count * capacity, local_width)

    picks = selected[0]
    experts = routes[:, 0]
    position = experts * capacity + slots_of(experts, expert_count)
    update = flat_back[position].astype(jnp.float32)
    result = arrived.astype(jnp.float32).at[picks].add(update)
    return result.astype(jnp.bfloat16)


def solution(mesh):
    placed = (
        P("section", "expert"),
        P("section"),
        P("section", None),
        P("section", None),
        P(None, "expert"),
        P("expert"),
        P("expert", "section", None),
        P("expert", "section", None),
        P("expert", "section", None),
    )
    return jax.shard_map(
        body, mesh=mesh, in_specs=placed, out_specs=P("section", "expert"), check_vma=False
    )
```

```python
import jax
import jax.numpy as jnp
from jax import lax
from jax.sharding import PartitionSpec as P


EPS = 1e-05


def passed_along(block, axis, distance):
    devices = range(lax.axis_size(axis))
    route = [((i - distance) % len(devices), i) for i in devices]
    return lax.ppermute(block, axis, route)


def feature_product(block, weight):
    return lax.dot_general(
        block, weight, (((1,), (1,)), ((), ())), preferred_element_type=jnp.float32
    )


def slots_of(experts, expert_count):
    onehot = (experts[:, None] == jnp.arange(expert_count, dtype=jnp.int32)[None, :]).astype(
        jnp.int32
    )
    ranks = jnp.cumsum(onehot, axis=0) - 1
    return jnp.sum(ranks * onehot, axis=1)


def body(activations, modality, selected, routes, norm_gain, router, gate_w, up_w, down_w):
    n_section = lax.axis_size("section")
    sel_count = selected.shape[1]
    expert_count = lax.axis_size("expert") * gate_w.shape[0]
    capacity = max(2, 3 * sel_count // (2 * expert_count))
    groups = n_section

    arrived = passed_along(activations, "section", 1)

    sel_next = passed_along(selected, "section", -1)[0]
    routes_next = passed_along(routes, "section", -1)[:, 0]
    rows = activations[sel_next]
    target = routes_next * capacity + slots_of(routes_next, expert_count)
    placing = (
        target[None, :] == jnp.arange(expert_count * capacity, dtype=jnp.int32)[:, None]
    ).astype(jnp.bfloat16)
    feature_width = rows.shape[1]
    buffer = jnp.dot(placing, rows, preferred_element_type=jnp.float32).astype(jnp.bfloat16)
    buffer = buffer.reshape(expert_count, capacity, feature_width)
    n_exp_dev = lax.axis_size("expert")
    local_width = router.shape[0]
    tables = jnp.concatenate([norm_gain, router[None, :]], axis=0)
    parts = []
    rest = tables
    for _ in range(3):
        piece = rest.astype(jnp.bfloat16)
        parts.append(piece)
        rest = rest - piece.astype(jnp.float32)
    table_rows = tables.shape[0]
    extra = jnp.broadcast_to(
        jnp.concatenate(parts, axis=0)[None], (expert_count, 3 * table_rows, local_width)
    )
    buffer = jnp.concatenate([buffer, extra], axis=1)
    mine = lax.all_to_all(buffer, "expert", split_axis=0, concat_axis=2, tiled=True)[0]
    arrived, mine = lax.optimization_barrier((arrived, mine))
    coded = mine[capacity:].astype(jnp.float32).reshape(3, table_rows, mine.shape[1])
    tables = (coded[0] + coded[1]) + coded[2]
    mine = mine[:capacity]

    gains_all = tables[:2]
    router_all = tables[2]
    expert_id = lax.axis_index("expert")
    kind = (expert_id >= expert_count // 2).astype(jnp.int32)
    gains = lax.dynamic_index_in_dim(gains_all, kind, axis=0, keepdims=False)
    picked = mine.astype(jnp.float32)
    d = picked.shape[1]
    scale = lax.rsqrt(jnp.sum(picked * picked, axis=1) / d + EPS)
    normed = (picked * scale[:, None] * gains[None, :]).astype(jnp.bfloat16)
    score = jax.nn.sigmoid(scale * jnp.sum(picked * gains[None, :] * router_all[None, :], axis=1))
    score_home = passed_along(score, "section", 1)

    block = lax.all_gather(normed, "section", axis=0, tiled=True)
    block, score_home = lax.optimization_barrier((block, score_home))
    gate = feature_product(block, gate_w[0])
    upper = feature_product(block, up_w[0])
    hidden = (jax.nn.silu(gate) * upper).astype(jnp.bfloat16)
    hidden_width = hidden.shape[1]
    hidden = jnp.roll(hidden.reshape(groups, capacity, hidden_width), 1, axis=0).reshape(
        groups * capacity, hidden_width
    )
    part = jnp.dot(hidden, down_w[0], preferred_element_type=jnp.float32)
    parts_in = lax.all_to_all(
        part.astype(jnp.bfloat16).reshape(groups, capacity, part.shape[1]),
        "section",
        split_axis=0,
        concat_axis=0,
        tiled=True,
    )
    summed = jnp.sum(parts_in.astype(jnp.float32), axis=0).astype(jnp.bfloat16)
    update_rows = (score_home[:, None] * summed.astype(jnp.float32)).astype(jnp.bfloat16)
    outgoing = update_rows.reshape(capacity, n_exp_dev, local_width).transpose(1, 0, 2)
    back = lax.all_to_all(outgoing, "expert", split_axis=0, concat_axis=0, tiled=True)
    flat_back = back.reshape(expert_count * capacity, local_width)

    picks = selected[0]
    experts = routes[:, 0]
    position = experts * capacity + slots_of(experts, expert_count)
    update = flat_back[position].astype(jnp.float32)
    result = arrived.astype(jnp.float32).at[picks].add(update)
    return result.astype(jnp.bfloat16)


def solution(mesh):
    placed = (
        P("section", "expert"),
        P("section"),
        P("section", None),
        P("section", None),
        P(None, "expert"),
        P("expert"),
        P("expert", "section", None),
        P("expert", "section", None),
        P("expert", "section", None),
    )
    return jax.shard_map(
        body, mesh=mesh, in_specs=placed, out_specs=P("section", "expert"), check_vma=False
    )
```

```python
import jax
import jax.numpy as jnp
from jax import lax
from jax.sharding import PartitionSpec as P


EPS = 1e-05


def passed_along(block, axis, distance):
    devices = range(lax.axis_size(axis))
    route = [((i - distance) % len(devices), i) for i in devices]
    return lax.ppermute(block, axis, route)


def feature_product(block, weight):
    return lax.dot_general(
        block, weight, (((1,), (1,)), ((), ())), preferred_element_type=jnp.float32
    )


def slots_of(experts, expert_count):
    onehot = (experts[:, None] == jnp.arange(expert_count, dtype=jnp.int32)[None, :]).astype(
        jnp.int32
    )
    ranks = jnp.cumsum(onehot, axis=0) - 1
    return jnp.sum(ranks * onehot, axis=1)


def body(activations, modality, selected, routes, norm_gain, router, gate_w, up_w, down_w):
    n_section = lax.axis_size("section")
    sel_count = selected.shape[1]
    expert_count = lax.axis_size("expert") * gate_w.shape[0]
    capacity = max(2, 3 * sel_count // (2 * expert_count))
    groups = n_section

    arrived = passed_along(activations, "section", 1)

    sel_next = passed_along(selected, "section", -1)[0]
    routes_next = passed_along(routes, "section", -1)[:, 0]
    rows = activations[sel_next]
    target = routes_next * capacity + slots_of(routes_next, expert_count)
    placing = (
        target[None, :] == jnp.arange(expert_count * capacity, dtype=jnp.int32)[:, None]
    ).astype(jnp.bfloat16)
    feature_width = rows.shape[1]
    buffer = jnp.dot(placing, rows, preferred_element_type=jnp.float32).astype(jnp.bfloat16)
    buffer = buffer.reshape(expert_count, capacity, feature_width)
    n_exp_dev = lax.axis_size("expert")
    local_width = router.shape[0]
    tables = jnp.concatenate([norm_gain, router[None, :]], axis=0)
    parts = []
    rest = tables
    for _ in range(3):
        piece = rest.astype(jnp.bfloat16)
        parts.append(piece)
        rest = rest - piece.astype(jnp.float32)
    table_rows = tables.shape[0]
    extra = jnp.broadcast_to(
        jnp.concatenate(parts, axis=0)[None], (expert_count, 3 * table_rows, local_width)
    )
    buffer = jnp.concatenate([buffer, extra], axis=1)
    mine = lax.all_to_all(buffer, "expert", split_axis=0, concat_axis=2, tiled=True)[0]
    arrived, mine = lax.optimization_barrier((arrived, mine))
    coded = mine[capacity:].astype(jnp.float32).reshape(3, table_rows, mine.shape[1])
    tables = (coded[0] + coded[1]) + coded[2]
    mine = mine[:capacity]

    gains_all = tables[:2]
    router_all = tables[2]
    expert_id = lax.axis_index("expert")
    kind = (expert_id >= expert_count // 2).astype(jnp.int32)
    gains = lax.dynamic_index_in_dim(gains_all, kind, axis=0, keepdims=False)
    picked = mine.astype(jnp.float32)
    d = picked.shape[1]
    scale = lax.rsqrt(jnp.sum(picked * picked, axis=1) / d + EPS)
    normed = (picked * scale[:, None] * gains[None, :]).astype(jnp.bfloat16)
    score = jax.nn.sigmoid(scale * jnp.sum(picked * gains[None, :] * router_all[None, :], axis=1))
    score_home = passed_along(score, "section", 1)

    half = d // 2
    block_a = lax.all_gather(normed[:, :half], "section", axis=0, tiled=True)
    block_b = lax.all_gather(normed[:, half:], "section", axis=0, tiled=True)
    block_a, score_home = lax.optimization_barrier((block_a, score_home))
    gate = feature_product(block_a, gate_w[0, :, :half]) + feature_product(block_b, gate_w[0, :, half:])
    upper = feature_product(block_a, up_w[0, :, :half]) + feature_product(block_b, up_w[0, :, half:])
    hidden = (jax.nn.silu(gate) * upper).astype(jnp.bfloat16)
    hidden_width = hidden.shape[1]
    hidden = jnp.roll(hidden.reshape(groups, capacity, hidden_width), 1, axis=0).reshape(
        groups * capacity, hidden_width
    )
    pieces = []
    for columns in (slice(0, half), slice(half, d)):
        part = jnp.dot(hidden, down_w[0, :, columns], preferred_element_type=jnp.float32)
        pieces.append(
            lax.psum_scatter(
                lax.optimization_barrier(part.astype(jnp.bfloat16))
                .astype(jnp.float32)
                .astype(jnp.bfloat16),
                "section",
                scatter_dimension=0,
                tiled=True,
            )
        )
    summed = jnp.concatenate(pieces, axis=1)
    update_rows = (score_home[:, None] * summed.astype(jnp.float32)).astype(jnp.bfloat16)
    outgoing = update_rows.reshape(capacity, n_exp_dev, local_width).transpose(1, 0, 2)
    back = lax.all_to_all(outgoing, "expert", split_axis=0, concat_axis=0, tiled=True)
    flat_back = back.reshape(expert_count * capacity, local_width)

    picks = selected[0]
    experts = routes[:, 0]
    position = experts * capacity + slots_of(experts, expert_count)
    update = flat_back[position].astype(jnp.float32)
    result = arrived.astype(jnp.float32).at[picks].add(update)
    return result.astype(jnp.bfloat16)


def solution(mesh):
    placed = (
        P("section", "expert"),
        P("section"),
        P("section", None),
        P("section", None),
        P(None, "expert"),
        P("expert"),
        P("expert", "section", None),
        P("expert", "section", None),
        P("expert", "section", None),
    )
    return jax.shard_map(
        body, mesh=mesh, in_specs=placed, out_specs=P("section", "expert"), check_vma=False
    )
```

```python
import jax
import jax.numpy as jnp
from jax import lax
from jax.sharding import PartitionSpec as P


EPS = 1e-05


def passed_along(block, axis, distance):
    devices = range(lax.axis_size(axis))
    route = [((i - distance) % len(devices), i) for i in devices]
    return lax.ppermute(block, axis, route)


def feature_product(block, weight):
    return lax.dot_general(
        block, weight, (((1,), (1,)), ((), ())), preferred_element_type=jnp.float32
    )


def slots_of(experts, expert_count):
    onehot = (experts[:, None] == jnp.arange(expert_count, dtype=jnp.int32)[None, :]).astype(
        jnp.int32
    )
    ranks = jnp.cumsum(onehot, axis=0) - 1
    return jnp.sum(ranks * onehot, axis=1)


def body(activations, modality, selected, routes, norm_gain, router, gate_w, up_w, down_w):
    n_section = lax.axis_size("section")
    sel_count = selected.shape[1]
    expert_count = lax.axis_size("expert") * gate_w.shape[0]
    capacity = max(2, 3 * sel_count // (2 * expert_count))
    groups = n_section

    arrived = passed_along(activations, "section", 1)

    sel_next = passed_along(selected, "section", -1)[0]
    routes_next = passed_along(routes, "section", -1)[:, 0]
    rows = activations[sel_next]
    target = routes_next * capacity + slots_of(routes_next, expert_count)
    placing = (
        target[None, :] == jnp.arange(expert_count * capacity, dtype=jnp.int32)[:, None]
    ).astype(jnp.bfloat16)
    feature_width = rows.shape[1]
    buffer = jnp.dot(placing, rows, preferred_element_type=jnp.float32).astype(jnp.bfloat16)
    buffer = buffer.reshape(expert_count, capacity, feature_width)
    n_exp_dev = lax.axis_size("expert")
    local_width = router.shape[0]
    tables = jnp.concatenate([norm_gain, router[None, :]], axis=0)
    parts = []
    rest = tables
    for _ in range(3):
        piece = rest.astype(jnp.bfloat16)
        parts.append(piece)
        rest = rest - piece.astype(jnp.float32)
    table_rows = tables.shape[0]
    extra = jnp.broadcast_to(
        jnp.concatenate(parts, axis=0)[None], (expert_count, 3 * table_rows, local_width)
    )
    buffer = jnp.concatenate([buffer, extra], axis=1)
    mine = lax.all_to_all(buffer, "expert", split_axis=0, concat_axis=2, tiled=True)[0]
    arrived, mine = lax.optimization_barrier((arrived, mine))
    coded = mine[capacity:].astype(jnp.float32).reshape(3, table_rows, mine.shape[1])
    tables = (coded[0] + coded[1]) + coded[2]
    mine = mine[:capacity]

    gains_all = tables[:2]
    router_all = tables[2]
    expert_id = lax.axis_index("expert")
    kind = (expert_id >= expert_count // 2).astype(jnp.int32)
    gains = lax.dynamic_index_in_dim(gains_all, kind, axis=0, keepdims=False)
    picked = mine.astype(jnp.float32)
    d = picked.shape[1]
    scale = lax.rsqrt(jnp.sum(picked * picked, axis=1) / d + EPS)
    normed = (picked * scale[:, None] * gains[None, :]).astype(jnp.bfloat16)
    score = jax.nn.sigmoid(scale * jnp.sum(picked * gains[None, :] * router_all[None, :], axis=1))
    score_home = passed_along(score, "section", 1)

    block = lax.all_gather(normed, "section", axis=0, tiled=True)
    block, score_home = lax.optimization_barrier((block, score_home))
    gate = feature_product(block, gate_w[0])
    upper = feature_product(block, up_w[0])
    hidden = (jax.nn.silu(gate) * upper).astype(jnp.bfloat16)
    hidden_width = hidden.shape[1]
    hidden = jnp.roll(hidden.reshape(groups, capacity, hidden_width), 1, axis=0).reshape(
        groups * capacity, hidden_width
    )
    part = jnp.dot(hidden, down_w[0], preferred_element_type=jnp.float32).astype(jnp.bfloat16)
    part = part.reshape(groups, capacity, part.shape[1])
    me = lax.axis_index("section")
    total = part[me].astype(jnp.float32)
    for shift in range(1, groups):
        outgoing_part = lax.dynamic_index_in_dim(part, (me + shift) % groups, axis=0, keepdims=False)
        total = total + passed_along(outgoing_part, "section", shift).astype(jnp.float32)
    summed = total.astype(jnp.bfloat16)
    update_rows = (score_home[:, None] * summed.astype(jnp.float32)).astype(jnp.bfloat16)
    outgoing = update_rows.reshape(capacity, n_exp_dev, local_width).transpose(1, 0, 2)
    back = lax.all_to_all(outgoing, "expert", split_axis=0, concat_axis=0, tiled=True)
    flat_back = back.reshape(expert_count * capacity, local_width)

    picks = selected[0]
    experts = routes[:, 0]
    position = experts * capacity + slots_of(experts, expert_count)
    update = flat_back[position].astype(jnp.float32)
    result = arrived.astype(jnp.float32).at[picks].add(update)
    return result.astype(jnp.bfloat16)


def solution(mesh):
    placed = (
        P("section", "expert"),
        P("section"),
        P("section", None),
        P("section", None),
        P(None, "expert"),
        P("expert"),
        P("expert", "section", None),
        P("expert", "section", None),
        P("expert", "section", None),
    )
    return jax.shard_map(
        body, mesh=mesh, in_specs=placed, out_specs=P("section", "expert"), check_vma=False
    )
```

```python
import jax
import jax.numpy as jnp
from jax import lax
from jax.sharding import PartitionSpec as P


EPS = 1e-05


def passed_along(block, axis, distance):
    devices = range(lax.axis_size(axis))
    route = [((i - distance) % len(devices), i) for i in devices]
    return lax.ppermute(block, axis, route)


def feature_product(block, weight):
    return lax.dot_general(
        block, weight, (((1,), (1,)), ((), ())), preferred_element_type=jnp.float32
    )


def body(activations, modality, selected, routes, norm_gain, router, gate_w, up_w, down_w):
    n_section = lax.axis_size("section")
    sel_count = selected.shape[1]
    expert_count = lax.axis_size("expert") * gate_w.shape[0]
    capacity = max(2, 3 * sel_count // (2 * expert_count))
    groups = n_section

    sel_next = passed_along(selected, "section", -1)[0]
    routes_next = passed_along(routes, "section", -1)[:, 0]
    rows = activations[sel_next]
    both = jnp.stack([routes_next, routes[:, 0]], axis=1)
    onehot = (both[:, :, None] == jnp.arange(expert_count, dtype=jnp.int32)[None, None, :]).astype(
        jnp.int32
    )
    slots = jnp.sum((jnp.cumsum(onehot, axis=0) - 1) * onehot, axis=2)
    targets = both * capacity + slots
    target = targets[:, 0]
    position = targets[:, 1]
    placing = (
        target[None, :] == jnp.arange(expert_count * capacity, dtype=jnp.int32)[:, None]
    ).astype(jnp.bfloat16)
    feature_width = rows.shape[1]
    buffer = jnp.dot(placing, rows, preferred_element_type=jnp.float32).astype(jnp.bfloat16)
    buffer = buffer.reshape(expert_count, capacity, feature_width)
    n_exp_dev = lax.axis_size("expert")
    local_width = router.shape[0]
    tables = jnp.concatenate([norm_gain, router[None, :]], axis=0)
    parts = []
    rest = tables
    for _ in range(3):
        piece = rest.astype(jnp.bfloat16)
        parts.append(piece)
        rest = rest - piece.astype(jnp.float32)
    table_rows = tables.shape[0]
    extra = jnp.broadcast_to(
        jnp.concatenate(parts, axis=0)[None], (expert_count, 3 * table_rows, local_width)
    )
    buffer = jnp.concatenate([buffer, extra], axis=1)
    mine = lax.all_to_all(buffer, "expert", split_axis=0, concat_axis=2, tiled=True)[0]
    coded = mine[capacity:].astype(jnp.float32).reshape(3, table_rows, mine.shape[1])
    tables = (coded[0] + coded[1]) + coded[2]
    mine = mine[:capacity]

    gains_all = tables[:2]
    router_all = tables[2]
    expert_id = lax.axis_index("expert")
    kind = (expert_id >= expert_count // 2).astype(jnp.int32)
    gains = lax.dynamic_index_in_dim(gains_all, kind, axis=0, keepdims=False)
    picked = mine.astype(jnp.float32)
    d = picked.shape[1]
    scale = lax.rsqrt(jnp.sum(picked * picked, axis=1) / d + EPS)
    normed = (picked * scale[:, None] * gains[None, :]).astype(jnp.bfloat16)
    score = jax.nn.sigmoid(scale * jnp.sum(picked * gains[None, :] * router_all[None, :], axis=1))
    score_home = passed_along(score, "section", 1)

    block = lax.all_gather(normed, "section", axis=0, tiled=True)
    block, score_home, leaving = lax.optimization_barrier((block, score_home, activations))
    arrived = passed_along(leaving, "section", 1)
    gate = feature_product(block, gate_w[0])
    upper = feature_product(block, up_w[0])
    hidden = (jax.nn.silu(gate) * upper).astype(jnp.bfloat16)
    hidden_width = hidden.shape[1]
    hidden = jnp.roll(hidden.reshape(groups, capacity, hidden_width), 1, axis=0).reshape(
        groups * capacity, hidden_width
    )
    part = jnp.dot(hidden, down_w[0], preferred_element_type=jnp.float32)
    summed = lax.psum_scatter(
        lax.optimization_barrier(part.astype(jnp.bfloat16))
        .astype(jnp.float32)
        .astype(jnp.bfloat16),
        "section",
        scatter_dimension=0,
        tiled=True,
    )
    update_rows = (score_home[:, None] * summed.astype(jnp.float32)).astype(jnp.bfloat16)
    outgoing = update_rows.reshape(capacity, n_exp_dev, local_width).transpose(1, 0, 2)
    back = lax.all_to_all(outgoing, "expert", split_axis=0, concat_axis=0, tiled=True)
    flat_back = back.reshape(expert_count * capacity, local_width)

    picks = selected[0]
    token_count = arrived.shape[0]
    source = jnp.full((token_count,), -1, jnp.int32).at[picks].set(position)
    spread = (
        source[:, None] == jnp.arange(expert_count * capacity, dtype=jnp.int32)[None, :]
    ).astype(jnp.bfloat16)
    update = jnp.dot(spread, flat_back, preferred_element_type=jnp.float32)
    return (arrived.astype(jnp.float32) + update).astype(jnp.bfloat16)


def solution(mesh):
    placed = (
        P("section", "expert"),
        P("section"),
        P("section", None),
        P("section", None),
        P(None, "expert"),
        P("expert"),
        P("expert", "section", None),
        P("expert", "section", None),
        P("expert", "section", None),
    )
    return jax.shard_map(
        body, mesh=mesh, in_specs=placed, out_specs=P("section", "expert"), check_vma=False
    )
```

```python
import jax
import jax.numpy as jnp
from jax import lax
from jax.sharding import PartitionSpec as P


EPS = 1e-05


def passed_along(block, axis, distance):
    devices = range(lax.axis_size(axis))
    route = [((i - distance) % len(devices), i) for i in devices]
    return lax.ppermute(block, axis, route)


def feature_product(block, weight):
    return lax.dot_general(
        block, weight, (((1,), (1,)), ((), ())), preferred_element_type=jnp.float32
    )


def body(activations, modality, selected, routes, norm_gain, router, gate_w, up_w, down_w):
    n_section = lax.axis_size("section")
    sel_count = selected.shape[1]
    expert_count = lax.axis_size("expert") * gate_w.shape[0]
    capacity = max(2, 3 * sel_count // (2 * expert_count))
    groups = n_section

    sel_next = passed_along(selected, "section", -1)[0]
    routes_next = passed_along(routes, "section", -1)[:, 0]
    rows = activations[sel_next]
    both = jnp.stack([routes_next, routes[:, 0]], axis=1)
    onehot = (both[:, :, None] == jnp.arange(expert_count, dtype=jnp.int32)[None, None, :]).astype(
        jnp.int32
    )
    slots = jnp.sum((jnp.cumsum(onehot, axis=0) - 1) * onehot, axis=2)
    targets = both * capacity + slots
    target = targets[:, 0]
    position = targets[:, 1]
    placing = (
        target[None, :] == jnp.arange(expert_count * capacity, dtype=jnp.int32)[:, None]
    ).astype(jnp.bfloat16)
    feature_width = rows.shape[1]
    buffer = jnp.dot(placing, rows, preferred_element_type=jnp.float32).astype(jnp.bfloat16)
    buffer = buffer.reshape(expert_count, capacity, feature_width)
    n_exp_dev = lax.axis_size("expert")
    local_width = router.shape[0]
    kinds = (jnp.arange(expert_count, dtype=jnp.int32) >= expert_count // 2).astype(jnp.int32)
    tables = jnp.stack(
        [norm_gain[kinds], jnp.broadcast_to(router[None, :], (expert_count, local_width))], axis=1
    )
    parts = []
    rest = tables
    for _ in range(3):
        piece = rest.astype(jnp.bfloat16)
        parts.append(piece)
        rest = rest - piece.astype(jnp.float32)
    table_rows = tables.shape[1]
    coded_rows = 3 * table_rows
    padded_rows = -(-coded_rows // 8) * 8
    parts.append(jnp.zeros((expert_count, padded_rows - coded_rows, local_width), jnp.bfloat16))
    buffer = jnp.concatenate([buffer] + parts, axis=1)
    mine = lax.all_to_all(buffer, "expert", split_axis=0, concat_axis=2, tiled=True)[0]
    coded = mine[capacity : capacity + coded_rows].astype(jnp.float32)
    coded = coded.reshape(3, table_rows, mine.shape[1])
    tables = (coded[0] + coded[1]) + coded[2]
    mine = mine[:capacity]

    gains = tables[0]
    router_all = tables[1]
    picked = mine.astype(jnp.float32)
    d = picked.shape[1]
    scale = lax.rsqrt(jnp.sum(picked * picked, axis=1) / d + EPS)
    normed = (picked * scale[:, None] * gains[None, :]).astype(jnp.bfloat16)
    score = jax.nn.sigmoid(scale * jnp.sum(picked * gains[None, :] * router_all[None, :], axis=1))
    score_home = passed_along(score, "section", 1)

    block = lax.all_gather(normed, "section", axis=0, tiled=True)
    block, score_home, leaving = lax.optimization_barrier((block, score_home, activations))
    arrived = passed_along(leaving, "section", 1)
    gate = feature_product(block, gate_w[0])
    upper = feature_product(block, up_w[0])
    hidden = (jax.nn.silu(gate) * upper).astype(jnp.bfloat16)
    hidden_width = hidden.shape[1]
    hidden = jnp.roll(hidden.reshape(groups, capacity, hidden_width), 1, axis=0).reshape(
        groups * capacity, hidden_width
    )
    part = jnp.dot(hidden, down_w[0], preferred_element_type=jnp.float32)
    summed = lax.psum_scatter(
        lax.optimization_barrier(part.astype(jnp.bfloat16))
        .astype(jnp.float32)
        .astype(jnp.bfloat16),
        "section",
        scatter_dimension=0,
        tiled=True,
    )
    update_rows = (score_home[:, None] * summed.astype(jnp.float32)).astype(jnp.bfloat16)
    outgoing = update_rows.reshape(capacity, n_exp_dev, local_width).transpose(1, 0, 2)
    back = lax.all_to_all(outgoing, "expert", split_axis=0, concat_axis=0, tiled=True)
    flat_back = back.reshape(expert_count * capacity, local_width)

    picks = selected[0]
    token_count = arrived.shape[0]
    source = jnp.full((token_count,), -1, jnp.int32).at[picks].set(position)
    spread = (
        source[:, None] == jnp.arange(expert_count * capacity, dtype=jnp.int32)[None, :]
    ).astype(jnp.bfloat16)
    update = jnp.dot(spread, flat_back, preferred_element_type=jnp.float32)
    return (arrived.astype(jnp.float32) + update).astype(jnp.bfloat16)


def solution(mesh):
    placed = (
        P("section", "expert"),
        P("section"),
        P("section", None),
        P("section", None),
        P(None, "expert"),
        P("expert"),
        P("expert", "section", None),
        P("expert", "section", None),
        P("expert", "section", None),
    )
    return jax.shard_map(
        body, mesh=mesh, in_specs=placed, out_specs=P("section", "expert"), check_vma=False
    )
```

```python
import jax
import jax.numpy as jnp
from jax import lax
from jax.sharding import PartitionSpec as P


EPS = 1e-05


SECTION = ("chip", "core")


def passed_along(block, axis, distance):
    names = axis if isinstance(axis, tuple) else (axis,)
    count = 1
    for name in names:
        count *= lax.axis_size(name)
    route = [((i - distance) % count, i) for i in range(count)]
    return lax.ppermute(block, axis, route)


def feature_product(block, weight):
    return lax.dot_general(
        block, weight, (((1,), (1,)), ((), ())), preferred_element_type=jnp.float32
    )


def body(activations, modality, selected, routes, norm_gain, router, gate_w, up_w, down_w):
    n_chip = lax.axis_size("chip")
    n_core = lax.axis_size("core")
    n_section = n_chip * n_core
    sel_count = selected.shape[1]
    expert_count = lax.axis_size("expert") * gate_w.shape[0]
    capacity = max(2, 3 * sel_count // (2 * expert_count))
    groups = n_section

    sel_next = passed_along(selected, SECTION, -1)[0]
    routes_next = passed_along(routes, SECTION, -1)[:, 0]
    rows = activations[sel_next]
    both = jnp.stack([routes_next, routes[:, 0]], axis=1)
    onehot = (both[:, :, None] == jnp.arange(expert_count, dtype=jnp.int32)[None, None, :]).astype(
        jnp.int32
    )
    slots = jnp.sum((jnp.cumsum(onehot, axis=0) - 1) * onehot, axis=2)
    targets = both * capacity + slots
    target = targets[:, 0]
    position = targets[:, 1]
    placing = (
        target[None, :] == jnp.arange(expert_count * capacity, dtype=jnp.int32)[:, None]
    ).astype(jnp.bfloat16)
    feature_width = rows.shape[1]
    buffer = jnp.dot(placing, rows, preferred_element_type=jnp.float32).astype(jnp.bfloat16)
    buffer = buffer.reshape(expert_count, capacity, feature_width)
    n_exp_dev = lax.axis_size("expert")
    local_width = router.shape[0]
    kinds = (jnp.arange(expert_count, dtype=jnp.int32) >= expert_count // 2).astype(jnp.int32)
    tables = jnp.stack(
        [norm_gain[kinds], jnp.broadcast_to(router[None, :], (expert_count, local_width))], axis=1
    )
    parts = []
    rest = tables
    for _ in range(3):
        piece = rest.astype(jnp.bfloat16)
        parts.append(piece)
        rest = rest - piece.astype(jnp.float32)
    table_rows = tables.shape[1]
    coded_rows = 3 * table_rows
    padded_rows = -(-coded_rows // 8) * 8
    parts.append(jnp.zeros((expert_count, padded_rows - coded_rows, local_width), jnp.bfloat16))
    buffer = jnp.concatenate([buffer] + parts, axis=1)
    mine = lax.all_to_all(buffer, "expert", split_axis=0, concat_axis=2, tiled=True)[0]
    coded = mine[capacity : capacity + coded_rows].astype(jnp.float32)
    coded = coded.reshape(3, table_rows, mine.shape[1])
    tables = (coded[0] + coded[1]) + coded[2]
    mine = mine[:capacity]

    gains = tables[0]
    router_all = tables[1]
    picked = mine.astype(jnp.float32)
    d = picked.shape[1]
    scale = lax.rsqrt(jnp.sum(picked * picked, axis=1) / d + EPS)
    normed = (picked * scale[:, None] * gains[None, :]).astype(jnp.bfloat16)
    score = jax.nn.sigmoid(scale * jnp.sum(picked * gains[None, :] * router_all[None, :], axis=1))
    score_home = passed_along(score, SECTION, 1)

    block = lax.all_gather(normed, SECTION, axis=0, tiled=True)
    block, score_home, leaving = lax.optimization_barrier((block, score_home, activations))
    arrived = passed_along(leaving, SECTION, 1)
    gate = feature_product(block, gate_w[0])
    upper = feature_product(block, up_w[0])
    hidden = (jax.nn.silu(gate) * upper).astype(jnp.bfloat16)
    hidden_width = hidden.shape[1]
    hidden = jnp.roll(hidden.reshape(groups, capacity, hidden_width), 1, axis=0).reshape(
        groups * capacity, hidden_width
    )
    part = jnp.dot(hidden, down_w[0], preferred_element_type=jnp.float32)
    pair = lax.psum_scatter(
        lax.optimization_barrier(part.astype(jnp.bfloat16))
        .astype(jnp.float32)
        .astype(jnp.bfloat16),
        "chip",
        scatter_dimension=0,
        tiled=True,
    ).reshape(n_core, capacity, part.shape[1])
    core = lax.axis_index("core")
    keep = lax.dynamic_index_in_dim(pair, core, axis=0, keepdims=False)
    give = lax.dynamic_index_in_dim(pair, 1 - core, axis=0, keepdims=False)
    taken = lax.ppermute(give, "core", [(0, 1), (1, 0)])
    summed = (keep.astype(jnp.float32) + taken.astype(jnp.float32)).astype(jnp.bfloat16)
    update_rows = (score_home[:, None] * summed.astype(jnp.float32)).astype(jnp.bfloat16)
    outgoing = update_rows.reshape(capacity, n_exp_dev, local_width).transpose(1, 0, 2)
    back = lax.all_to_all(outgoing, "expert", split_axis=0, concat_axis=0, tiled=True)
    flat_back = back.reshape(expert_count * capacity, local_width)

    picks = selected[0]
    token_count = arrived.shape[0]
    source = jnp.full((token_count,), -1, jnp.int32).at[picks].set(position)
    spread = (
        source[:, None] == jnp.arange(expert_count * capacity, dtype=jnp.int32)[None, :]
    ).astype(jnp.bfloat16)
    update = jnp.dot(spread, flat_back, preferred_element_type=jnp.float32)
    return (arrived.astype(jnp.float32) + update).astype(jnp.bfloat16)


def solution(mesh):
    n_section, n_expert = mesh.devices.shape
    split = jax.sharding.Mesh(
        mesh.devices.reshape(n_section // 2, 2, n_expert), ("chip", "core", "expert")
    )
    placed = (
        P(SECTION, "expert"),
        P(SECTION),
        P(SECTION, None),
        P(SECTION, None),
        P(None, "expert"),
        P("expert"),
        P("expert", SECTION, None),
        P("expert", SECTION, None),
        P("expert", SECTION, None),
    )
    return jax.shard_map(
        body, mesh=split, in_specs=placed, out_specs=P(SECTION, "expert"), check_vma=False
    )
```

```python
import jax
import jax.numpy as jnp
from jax import lax
from jax.sharding import PartitionSpec as P


EPS = 1e-05


SECTION = ("chip", "core")


def passed_along(block, axis, distance):
    names = axis if isinstance(axis, tuple) else (axis,)
    count = 1
    for name in names:
        count *= lax.axis_size(name)
    route = [((i - distance) % count, i) for i in range(count)]
    return lax.ppermute(block, axis, route)


def feature_product(block, weight):
    return lax.dot_general(
        block, weight, (((1,), (1,)), ((), ())), preferred_element_type=jnp.float32
    )


def body(activations, modality, selected, routes, norm_gain, router, gate_w, up_w, down_w):
    n_chip = lax.axis_size("chip")
    n_core = lax.axis_size("core")
    n_section = n_chip * n_core
    sel_count = selected.shape[1]
    expert_count = lax.axis_size("expert") * gate_w.shape[0]
    capacity = max(2, 3 * sel_count // (2 * expert_count))
    groups = n_section

    sel_next = passed_along(selected, SECTION, -1)[0]
    routes_next = passed_along(routes, SECTION, -1)[:, 0]
    rows = activations[sel_next]
    both = jnp.stack([routes_next, routes[:, 0]], axis=1)
    onehot = (both[:, :, None] == jnp.arange(expert_count, dtype=jnp.int32)[None, None, :]).astype(
        jnp.int32
    )
    slots = jnp.sum((jnp.cumsum(onehot, axis=0) - 1) * onehot, axis=2)
    targets = both * capacity + slots
    target = targets[:, 0]
    position = targets[:, 1]
    placing = (
        target[None, :] == jnp.arange(expert_count * capacity, dtype=jnp.int32)[:, None]
    ).astype(jnp.bfloat16)
    feature_width = rows.shape[1]
    buffer = jnp.dot(placing, rows, preferred_element_type=jnp.float32).astype(jnp.bfloat16)
    buffer = buffer.reshape(expert_count, capacity, feature_width)
    n_exp_dev = lax.axis_size("expert")
    local_width = router.shape[0]
    kinds = (jnp.arange(expert_count, dtype=jnp.int32) >= expert_count // 2).astype(jnp.int32)
    tables = jnp.stack(
        [norm_gain[kinds], jnp.broadcast_to(router[None, :], (expert_count, local_width))], axis=1
    )
    parts = []
    rest = tables
    for _ in range(3):
        piece = rest.astype(jnp.bfloat16)
        parts.append(piece)
        rest = rest - piece.astype(jnp.float32)
    table_rows = tables.shape[1]
    coded_rows = 3 * table_rows
    padded_rows = -(-coded_rows // 8) * 8
    parts.append(jnp.zeros((expert_count, padded_rows - coded_rows, local_width), jnp.bfloat16))
    buffer = jnp.concatenate([buffer] + parts, axis=1)
    mine = lax.all_to_all(buffer, "expert", split_axis=0, concat_axis=2, tiled=True)[0]
    coded = mine[capacity : capacity + coded_rows].astype(jnp.float32)
    coded = coded.reshape(3, table_rows, mine.shape[1])
    tables = (coded[0] + coded[1]) + coded[2]
    mine = mine[:capacity]

    gains = tables[0]
    router_all = tables[1]
    picked = mine.astype(jnp.float32)
    d = picked.shape[1]
    scale = lax.rsqrt(jnp.sum(picked * picked, axis=1) / d + EPS)
    normed = (picked * scale[:, None] * gains[None, :]).astype(jnp.bfloat16)
    score = jax.nn.sigmoid(scale * jnp.sum(picked * gains[None, :] * router_all[None, :], axis=1))
    score_home = passed_along(score, SECTION, 1)

    block = lax.all_gather(normed, SECTION, axis=0, tiled=True)
    block, score_home, leaving = lax.optimization_barrier((block, score_home, activations))
    arrived = passed_along(leaving, SECTION, 1)
    gate = feature_product(block, gate_w[0])
    upper = feature_product(block, up_w[0])
    hidden = (jax.nn.silu(gate) * upper).astype(jnp.bfloat16)
    hidden_width = hidden.shape[1]
    order = []
    for core in range(n_core):
        for chip in range(n_chip):
            order.append((chip * n_core + core - 1) % n_section)
    hidden = jnp.take(
        hidden.reshape(groups, capacity, hidden_width), jnp.array(order, jnp.int32), axis=0
    ).reshape(groups * capacity, hidden_width)
    part = jnp.dot(hidden, down_w[0], preferred_element_type=jnp.float32)
    part = lax.optimization_barrier(part.astype(jnp.bfloat16)).astype(jnp.float32).astype(jnp.bfloat16)
    part = part.reshape(n_core, n_chip, capacity, part.shape[1])
    core = lax.axis_index("core")
    keep = lax.dynamic_index_in_dim(part, core, axis=0, keepdims=False)
    give = lax.dynamic_index_in_dim(part, 1 - core, axis=0, keepdims=False)
    taken = lax.ppermute(give, "core", [(0, 1), (1, 0)])
    pair = (keep.astype(jnp.float32) + taken.astype(jnp.float32)).astype(jnp.bfloat16)
    summed = lax.psum_scatter(
        pair.reshape(n_chip * capacity, part.shape[3]), "chip", scatter_dimension=0, tiled=True
    )
    update_rows = (score_home[:, None] * summed.astype(jnp.float32)).astype(jnp.bfloat16)
    outgoing = update_rows.reshape(capacity, n_exp_dev, local_width).transpose(1, 0, 2)
    back = lax.all_to_all(outgoing, "expert", split_axis=0, concat_axis=0, tiled=True)
    flat_back = back.reshape(expert_count * capacity, local_width)

    picks = selected[0]
    token_count = arrived.shape[0]
    source = jnp.full((token_count,), -1, jnp.int32).at[picks].set(position)
    spread = (
        source[:, None] == jnp.arange(expert_count * capacity, dtype=jnp.int32)[None, :]
    ).astype(jnp.bfloat16)
    update = jnp.dot(spread, flat_back, preferred_element_type=jnp.float32)
    return (arrived.astype(jnp.float32) + update).astype(jnp.bfloat16)


def solution(mesh):
    n_section, n_expert = mesh.devices.shape
    split = jax.sharding.Mesh(
        mesh.devices.reshape(n_section // 2, 2, n_expert), ("chip", "core", "expert")
    )
    placed = (
        P(SECTION, "expert"),
        P(SECTION),
        P(SECTION, None),
        P(SECTION, None),
        P(None, "expert"),
        P("expert"),
        P("expert", SECTION, None),
        P("expert", SECTION, None),
        P("expert", SECTION, None),
    )
    return jax.shard_map(
        body, mesh=split, in_specs=placed, out_specs=P(SECTION, "expert"), check_vma=False
    )
```

```python
import jax
import jax.numpy as jnp
from jax import lax
from jax.sharding import PartitionSpec as P


EPS = 1e-05


SECTION = ("chip", "core")


def passed_along(block, axis, distance):
    names = axis if isinstance(axis, tuple) else (axis,)
    count = 1
    for name in names:
        count *= lax.axis_size(name)
    route = [((i - distance) % count, i) for i in range(count)]
    return lax.ppermute(block, axis, route)


def feature_product(block, weight):
    return lax.dot_general(
        block, weight, (((1,), (1,)), ((), ())), preferred_element_type=jnp.float32
    )


def body(activations, modality, selected, routes, norm_gain, router, gate_w, up_w, down_w):
    n_chip = lax.axis_size("chip")
    n_core = lax.axis_size("core")
    n_section = n_chip * n_core
    sel_count = selected.shape[1]
    expert_count = lax.axis_size("expert") * gate_w.shape[0]
    capacity = max(2, 3 * sel_count // (2 * expert_count))
    groups = n_section

    sel_next = passed_along(selected, SECTION, -1)[0]
    routes_next = passed_along(routes, SECTION, -1)[:, 0]
    rows = activations[sel_next]
    both = jnp.stack([routes_next, routes[:, 0]], axis=1)
    onehot = (both[:, :, None] == jnp.arange(expert_count, dtype=jnp.int32)[None, None, :]).astype(
        jnp.int32
    )
    slots = jnp.sum((jnp.cumsum(onehot, axis=0) - 1) * onehot, axis=2)
    targets = both * capacity + slots
    target = targets[:, 0]
    position = targets[:, 1]
    placing = (
        target[None, :] == jnp.arange(expert_count * capacity, dtype=jnp.int32)[:, None]
    ).astype(jnp.bfloat16)
    feature_width = rows.shape[1]
    buffer = jnp.dot(placing, rows, preferred_element_type=jnp.float32).astype(jnp.bfloat16)
    buffer = buffer.reshape(expert_count, capacity, feature_width)
    n_exp_dev = lax.axis_size("expert")
    local_width = router.shape[0]
    kinds = (jnp.arange(expert_count, dtype=jnp.int32) >= expert_count // 2).astype(jnp.int32)
    tables = jnp.stack(
        [norm_gain[kinds], jnp.broadcast_to(router[None, :], (expert_count, local_width))], axis=1
    )
    parts = []
    rest = tables
    for _ in range(3):
        piece = rest.astype(jnp.bfloat16)
        parts.append(piece)
        rest = rest - piece.astype(jnp.float32)
    table_rows = tables.shape[1]
    coded_rows = 3 * table_rows
    padded_rows = -(-coded_rows // 8) * 8
    parts.append(jnp.zeros((expert_count, padded_rows - coded_rows, local_width), jnp.bfloat16))
    buffer = jnp.concatenate([buffer] + parts, axis=1)
    mine = lax.all_to_all(buffer, "expert", split_axis=0, concat_axis=2, tiled=True)[0]
    coded = mine[capacity : capacity + coded_rows].astype(jnp.float32)
    coded = coded.reshape(3, table_rows, mine.shape[1])
    tables = (coded[0] + coded[1]) + coded[2]
    mine = mine[:capacity]

    gains = tables[0]
    router_all = tables[1]
    picked = mine.astype(jnp.float32)
    d = picked.shape[1]
    scale = lax.rsqrt(jnp.sum(picked * picked, axis=1) / d + EPS)
    normed = (picked * scale[:, None] * gains[None, :]).astype(jnp.bfloat16)
    score = jax.nn.sigmoid(scale * jnp.sum(picked * gains[None, :] * router_all[None, :], axis=1))
    score_home = passed_along(score, SECTION, 1)

    block = lax.all_gather(normed, SECTION, axis=0, tiled=True)
    block, score_home, leaving = lax.optimization_barrier((block, score_home, activations))
    arrived = passed_along(leaving, SECTION, 1)
    gate = feature_product(block, gate_w[0])
    upper = feature_product(block, up_w[0])
    hidden = (jax.nn.silu(gate) * upper).astype(jnp.bfloat16)
    hidden_width = hidden.shape[1]
    order = []
    for core in range(n_core):
        for chip in range(n_chip):
            order.append((chip * n_core + core - 1) % n_section)
    hidden = jnp.take(
        hidden.reshape(groups, capacity, hidden_width), jnp.array(order, jnp.int32), axis=0
    ).reshape(groups * capacity, hidden_width)
    hidden = hidden.reshape(n_core, n_chip * capacity, hidden_width)
    core = lax.axis_index("core")

    def down_part(rows):
        part = jnp.dot(rows, down_w[0], preferred_element_type=jnp.float32)
        return lax.optimization_barrier(part.astype(jnp.bfloat16)).astype(jnp.float32).astype(jnp.bfloat16)

    give = down_part(lax.dynamic_index_in_dim(hidden, 1 - core, axis=0, keepdims=False))
    taken = lax.ppermute(give, "core", [(0, 1), (1, 0)])
    keep = down_part(lax.dynamic_index_in_dim(hidden, core, axis=0, keepdims=False))
    pair = (keep.astype(jnp.float32) + taken.astype(jnp.float32)).astype(jnp.bfloat16)
    summed = lax.psum_scatter(pair, "chip", scatter_dimension=0, tiled=True)
    update_rows = (score_home[:, None] * summed.astype(jnp.float32)).astype(jnp.bfloat16)
    outgoing = update_rows.reshape(capacity, n_exp_dev, local_width).transpose(1, 0, 2)
    back = lax.all_to_all(outgoing, "expert", split_axis=0, concat_axis=0, tiled=True)
    flat_back = back.reshape(expert_count * capacity, local_width)

    picks = selected[0]
    token_count = arrived.shape[0]
    source = jnp.full((token_count,), -1, jnp.int32).at[picks].set(position)
    spread = (
        source[:, None] == jnp.arange(expert_count * capacity, dtype=jnp.int32)[None, :]
    ).astype(jnp.bfloat16)
    update = jnp.dot(spread, flat_back, preferred_element_type=jnp.float32)
    return (arrived.astype(jnp.float32) + update).astype(jnp.bfloat16)


def solution(mesh):
    n_section, n_expert = mesh.devices.shape
    split = jax.sharding.Mesh(
        mesh.devices.reshape(n_section // 2, 2, n_expert), ("chip", "core", "expert")
    )
    placed = (
        P(SECTION, "expert"),
        P(SECTION),
        P(SECTION, None),
        P(SECTION, None),
        P(None, "expert"),
        P("expert"),
        P("expert", SECTION, None),
        P("expert", SECTION, None),
        P("expert", SECTION, None),
    )
    return jax.shard_map(
        body, mesh=split, in_specs=placed, out_specs=P(SECTION, "expert"), check_vma=False
    )
```

```python
import jax
import jax.numpy as jnp
from jax import lax
from jax.sharding import PartitionSpec as P


EPS = 1e-05


SECTION = ("chip", "core")


def passed_along(block, axis, distance):
    names = axis if isinstance(axis, tuple) else (axis,)
    count = 1
    for name in names:
        count *= lax.axis_size(name)
    route = [((i - distance) % count, i) for i in range(count)]
    return lax.ppermute(block, axis, route)


def feature_product(block, weight):
    return lax.dot_general(
        block, weight, (((1,), (1,)), ((), ())), preferred_element_type=jnp.float32
    )


def body(activations, modality, selected, routes, norm_gain, router, gate_w, up_w, down_w):
    n_chip = lax.axis_size("chip")
    n_core = lax.axis_size("core")
    n_section = n_chip * n_core
    sel_count = selected.shape[1]
    expert_count = lax.axis_size("expert") * gate_w.shape[0]
    capacity = max(2, 3 * sel_count // (2 * expert_count))
    groups = n_section

    sel_next = passed_along(selected, SECTION, -1)[0]
    routes_next = passed_along(routes, SECTION, -1)[:, 0]
    rows = activations[sel_next]
    both = jnp.stack([routes_next, routes[:, 0]], axis=1)
    onehot = (both[:, :, None] == jnp.arange(expert_count, dtype=jnp.int32)[None, None, :]).astype(
        jnp.int32
    )
    slots = jnp.sum((jnp.cumsum(onehot, axis=0) - 1) * onehot, axis=2)
    targets = both * capacity + slots
    target = targets[:, 0]
    position = targets[:, 1]
    feature_width = rows.shape[1]
    n_exp_dev = lax.axis_size("expert")
    local_width = router.shape[0]
    tables = jnp.concatenate([norm_gain, router[None, :]], axis=0)
    table_count = tables.shape[0]
    parts = []
    rest = tables
    for _ in range(3):
        piece = rest.astype(jnp.bfloat16)
        parts.append(piece)
        rest = rest - piece.astype(jnp.float32)
    sources = jnp.concatenate([rows] + parts, axis=0)
    table_rows = 2
    coded_rows = 3 * table_rows
    span = capacity + -(-coded_rows // 8) * 8
    slot_of_row = jnp.arange(expert_count * span, dtype=jnp.int32)
    row_expert = slot_of_row // span
    row_slot = slot_of_row % span
    row_kind = (row_expert >= expert_count // 2).astype(jnp.int32)
    coded_index = row_slot - capacity
    part_index = coded_index // table_rows
    table_index = jnp.where(coded_index % table_rows == 0, row_kind, table_count - 1)
    wanted = jnp.where(row_slot < capacity, row_expert * capacity + row_slot, -1)
    token_hit = target[None, :] == wanted[:, None]
    table_source = jnp.where(
        (coded_index >= 0) & (coded_index < coded_rows), part_index * table_count + table_index, -1
    )
    table_hit = table_source[:, None] == jnp.arange(3 * table_count, dtype=jnp.int32)[None, :]
    placing = jnp.concatenate([token_hit, table_hit], axis=1).astype(jnp.bfloat16)
    buffer = jnp.dot(placing, sources, preferred_element_type=jnp.float32).astype(jnp.bfloat16)
    buffer = buffer.reshape(expert_count, span, feature_width)
    mine = lax.all_to_all(buffer, "expert", split_axis=0, concat_axis=2, tiled=True)[0]
    coded = mine[capacity : capacity + coded_rows].astype(jnp.float32)
    coded = coded.reshape(3, table_rows, mine.shape[1])
    tables = (coded[0] + coded[1]) + coded[2]
    mine = mine[:capacity]

    gains = tables[0]
    router_all = tables[1]
    picked = mine.astype(jnp.float32)
    d = picked.shape[1]
    scale = lax.rsqrt(jnp.sum(picked * picked, axis=1) / d + EPS)
    normed = (picked * scale[:, None] * gains[None, :]).astype(jnp.bfloat16)
    score = jax.nn.sigmoid(scale * jnp.sum(picked * gains[None, :] * router_all[None, :], axis=1))
    score_home = passed_along(score, SECTION, 1)

    block = lax.all_gather(normed, SECTION, axis=0, tiled=True)
    block, score_home, leaving = lax.optimization_barrier((block, score_home, activations))
    arrived = passed_along(leaving, SECTION, 1)
    gate = feature_product(block, gate_w[0])
    upper = feature_product(block, up_w[0])
    hidden = (jax.nn.silu(gate) * upper).astype(jnp.bfloat16)
    hidden_width = hidden.shape[1]
    order = []
    for core in range(n_core):
        for chip in range(n_chip):
            order.append((chip * n_core + core - 1) % n_section)
    hidden = jnp.take(
        hidden.reshape(groups, capacity, hidden_width), jnp.array(order, jnp.int32), axis=0
    ).reshape(groups * capacity, hidden_width)
    hidden = hidden.reshape(n_core, n_chip * capacity, hidden_width)
    core = lax.axis_index("core")

    def down_part(rows):
        part = jnp.dot(rows, down_w[0], preferred_element_type=jnp.float32)
        return lax.optimization_barrier(part.astype(jnp.bfloat16)).astype(jnp.float32).astype(jnp.bfloat16)

    give = down_part(lax.dynamic_index_in_dim(hidden, 1 - core, axis=0, keepdims=False))
    taken = lax.ppermute(give, "core", [(0, 1), (1, 0)])
    keep = down_part(lax.dynamic_index_in_dim(hidden, core, axis=0, keepdims=False))
    pair = (keep.astype(jnp.float32) + taken.astype(jnp.float32)).astype(jnp.bfloat16)
    summed = lax.psum_scatter(pair, "chip", scatter_dimension=0, tiled=True)
    update_rows = (score_home[:, None] * summed.astype(jnp.float32)).astype(jnp.bfloat16)
    outgoing = update_rows.reshape(capacity, n_exp_dev, local_width).transpose(1, 0, 2)
    back = lax.all_to_all(outgoing, "expert", split_axis=0, concat_axis=0, tiled=True)
    flat_back = back.reshape(expert_count * capacity, local_width)

    picks = selected[0]
    token_count = arrived.shape[0]
    source = jnp.full((token_count,), -1, jnp.int32).at[picks].set(position)
    spread = (
        source[:, None] == jnp.arange(expert_count * capacity, dtype=jnp.int32)[None, :]
    ).astype(jnp.bfloat16)
    update = jnp.dot(spread, flat_back, preferred_element_type=jnp.float32)
    return (arrived.astype(jnp.float32) + update).astype(jnp.bfloat16)


def solution(mesh):
    n_section, n_expert = mesh.devices.shape
    split = jax.sharding.Mesh(
        mesh.devices.reshape(n_section // 2, 2, n_expert), ("chip", "core", "expert")
    )
    placed = (
        P(SECTION, "expert"),
        P(SECTION),
        P(SECTION, None),
        P(SECTION, None),
        P(None, "expert"),
        P("expert"),
        P("expert", SECTION, None),
        P("expert", SECTION, None),
        P("expert", SECTION, None),
    )
    return jax.shard_map(
        body, mesh=split, in_specs=placed, out_specs=P(SECTION, "expert"), check_vma=False
    )
```

```python
import jax
import jax.numpy as jnp
from jax import lax
from jax.sharding import PartitionSpec as P


EPS = 1e-05


SECTION = ("chip", "core")


def passed_along(block, axis, distance):
    names = axis if isinstance(axis, tuple) else (axis,)
    count = 1
    for name in names:
        count *= lax.axis_size(name)
    route = [((i - distance) % count, i) for i in range(count)]
    return lax.ppermute(block, axis, route)


def feature_product(block, weight):
    return lax.dot_general(
        block, weight, (((1,), (1,)), ((), ())), preferred_element_type=jnp.float32
    )


def body(activations, modality, selected, routes, norm_gain, router, gate_w, up_w, down_w):
    n_chip = lax.axis_size("chip")
    n_core = lax.axis_size("core")
    n_section = n_chip * n_core
    sel_count = selected.shape[1]
    expert_count = lax.axis_size("expert") * gate_w.shape[0]
    capacity = max(2, 3 * sel_count // (2 * expert_count))
    groups = n_section

    sel_next = passed_along(selected, SECTION, -1)[0]
    routes_next = passed_along(routes, SECTION, -1)[:, 0]
    rows = activations[sel_next]
    both = jnp.stack([routes_next, routes[:, 0]], axis=1)
    onehot = (both[:, :, None] == jnp.arange(expert_count, dtype=jnp.int32)[None, None, :]).astype(
        jnp.int32
    )
    slots = jnp.sum((jnp.cumsum(onehot, axis=0) - 1) * onehot, axis=2)
    targets = both * capacity + slots
    target = targets[:, 0]
    position = targets[:, 1]
    feature_width = rows.shape[1]
    n_exp_dev = lax.axis_size("expert")
    local_width = router.shape[0]
    tables = jnp.concatenate([norm_gain, router[None, :]], axis=0)
    table_count = tables.shape[0]
    parts = []
    rest = tables
    for _ in range(3):
        piece = rest.astype(jnp.bfloat16)
        parts.append(piece)
        rest = rest - piece.astype(jnp.float32)
    sources = jnp.concatenate([rows] + parts, axis=0)
    table_rows = 2
    coded_rows = 3 * table_rows
    span = capacity + -(-coded_rows // 8) * 8
    slot_of_row = jnp.arange(expert_count * span, dtype=jnp.int32)
    row_expert = slot_of_row // span
    row_slot = slot_of_row % span
    row_kind = (row_expert >= expert_count // 2).astype(jnp.int32)
    coded_index = row_slot - capacity
    part_index = coded_index // table_rows
    table_index = jnp.where(coded_index % table_rows == 0, row_kind, table_count - 1)
    wanted = jnp.where(row_slot < capacity, row_expert * capacity + row_slot, -1)
    token_hit = target[None, :] == wanted[:, None]
    table_source = jnp.where(
        (coded_index >= 0) & (coded_index < coded_rows), part_index * table_count + table_index, -1
    )
    table_hit = table_source[:, None] == jnp.arange(3 * table_count, dtype=jnp.int32)[None, :]
    placing = jnp.concatenate([token_hit, table_hit], axis=1).astype(jnp.bfloat16)
    buffer = jnp.dot(placing, sources, preferred_element_type=jnp.float32).astype(jnp.bfloat16)
    buffer = buffer.reshape(expert_count, span, feature_width)
    mine = lax.all_to_all(buffer, "expert", split_axis=0, concat_axis=2, tiled=True)[0]
    coded = mine[capacity : capacity + coded_rows].astype(jnp.float32)
    coded = coded.reshape(3, table_rows, mine.shape[1])
    tables = (coded[0] + coded[1]) + coded[2]
    mine = mine[:capacity]

    gains = tables[0]
    router_all = tables[1]
    picked = mine.astype(jnp.float32)
    d = picked.shape[1]
    scale = lax.rsqrt(jnp.sum(picked * picked, axis=1) / d + EPS)
    normed = (picked * scale[:, None] * gains[None, :]).astype(jnp.bfloat16)
    score = jax.nn.sigmoid(scale * jnp.sum(picked * gains[None, :] * router_all[None, :], axis=1))
    score_home = passed_along(score, SECTION, 1)

    block = lax.all_gather(normed, SECTION, axis=0, tiled=True)
    block, score_home, leaving = lax.optimization_barrier((block, score_home, activations))
    arrived = passed_along(leaving, SECTION, 1)
    gate = feature_product(block, gate_w[0])
    upper = feature_product(block, up_w[0])
    hidden = (jax.nn.silu(gate) * upper).astype(jnp.bfloat16)
    hidden_width = hidden.shape[1]
    order = []
    for core in range(n_core):
        for chip in range(n_chip):
            order.append((chip * n_core + core - 1) % n_section)
    hidden = jnp.take(
        hidden.reshape(groups, capacity, hidden_width), jnp.array(order, jnp.int32), axis=0
    ).reshape(groups * capacity, hidden_width)
    hidden = hidden.reshape(n_core, n_chip * capacity, hidden_width)
    core = lax.axis_index("core")

    def down_part(rows):
        part = jnp.dot(rows, down_w[0], preferred_element_type=jnp.float32)
        return lax.optimization_barrier(part.astype(jnp.bfloat16)).astype(jnp.float32).astype(jnp.bfloat16)

    give = down_part(lax.dynamic_index_in_dim(hidden, 1 - core, axis=0, keepdims=False))
    taken = lax.ppermute(give, "core", [(0, 1), (1, 0)])
    keep = jnp.dot(
        lax.dynamic_index_in_dim(hidden, core, axis=0, keepdims=False),
        down_w[0],
        preferred_element_type=jnp.float32,
    )
    pair = (keep + taken.astype(jnp.float32)).astype(jnp.bfloat16)
    summed = lax.psum_scatter(pair, "chip", scatter_dimension=0, tiled=True)
    update_rows = (score_home[:, None] * summed.astype(jnp.float32)).astype(jnp.bfloat16)
    outgoing = update_rows.reshape(capacity, n_exp_dev, local_width).transpose(1, 0, 2)
    back = lax.all_to_all(outgoing, "expert", split_axis=0, concat_axis=0, tiled=True)
    flat_back = back.reshape(expert_count * capacity, local_width)

    picks = selected[0]
    token_count = arrived.shape[0]
    source = jnp.full((token_count,), -1, jnp.int32).at[picks].set(position)
    spread = (
        source[:, None] == jnp.arange(expert_count * capacity, dtype=jnp.int32)[None, :]
    ).astype(jnp.bfloat16)
    update = jnp.dot(spread, flat_back, preferred_element_type=jnp.float32)
    return (arrived.astype(jnp.float32) + update).astype(jnp.bfloat16)


def solution(mesh):
    n_section, n_expert = mesh.devices.shape
    split = jax.sharding.Mesh(
        mesh.devices.reshape(n_section // 2, 2, n_expert), ("chip", "core", "expert")
    )
    placed = (
        P(SECTION, "expert"),
        P(SECTION),
        P(SECTION, None),
        P(SECTION, None),
        P(None, "expert"),
        P("expert"),
        P("expert", SECTION, None),
        P("expert", SECTION, None),
        P("expert", SECTION, None),
    )
    return jax.shard_map(
        body, mesh=split, in_specs=placed, out_specs=P(SECTION, "expert"), check_vma=False
    )
```

```python
import jax
import jax.numpy as jnp
from jax import lax
from jax.sharding import PartitionSpec as P


EPS = 1e-05


SECTION = ("chip", "core")


def passed_along(block, axis, distance):
    names = axis if isinstance(axis, tuple) else (axis,)
    count = 1
    for name in names:
        count *= lax.axis_size(name)
    route = [((i - distance) % count, i) for i in range(count)]
    return lax.ppermute(block, axis, route)


def feature_product(block, weight):
    return lax.dot_general(
        block, weight, (((1,), (1,)), ((), ())), preferred_element_type=jnp.float32
    )


def body(activations, modality, selected, routes, norm_gain, router, gate_w, up_w, down_w):
    n_chip = lax.axis_size("chip")
    n_core = lax.axis_size("core")
    n_section = n_chip * n_core
    sel_count = selected.shape[1]
    expert_count = lax.axis_size("expert") * gate_w.shape[0]
    capacity = max(2, 3 * sel_count // (2 * expert_count))
    groups = n_section

    sel_next = passed_along(selected, SECTION, -1)[0]
    routes_next = passed_along(routes, SECTION, -1)[:, 0]
    rows = activations[sel_next]
    both = jnp.stack([routes_next, routes[:, 0]], axis=1)
    onehot = (both[:, :, None] == jnp.arange(expert_count, dtype=jnp.int32)[None, None, :]).astype(
        jnp.int32
    )
    slots = jnp.sum((jnp.cumsum(onehot, axis=0) - 1) * onehot, axis=2)
    targets = both * capacity + slots
    target = targets[:, 0]
    position = targets[:, 1]
    feature_width = rows.shape[1]
    n_exp_dev = lax.axis_size("expert")
    local_width = router.shape[0]
    tables = jnp.concatenate([norm_gain, router[None, :]], axis=0)
    table_count = tables.shape[0]
    parts = []
    rest = tables
    for _ in range(3):
        piece = rest.astype(jnp.bfloat16)
        parts.append(piece)
        rest = rest - piece.astype(jnp.float32)
    sources = jnp.concatenate([rows] + parts, axis=0)
    table_rows = 2
    coded_rows = 3 * table_rows
    span = capacity + -(-coded_rows // 8) * 8
    slot_of_row = jnp.arange(expert_count * span, dtype=jnp.int32)
    row_expert = slot_of_row // span
    row_slot = slot_of_row % span
    row_kind = (row_expert >= expert_count // 2).astype(jnp.int32)
    coded_index = row_slot - capacity
    part_index = coded_index // table_rows
    table_index = jnp.where(coded_index % table_rows == 0, row_kind, table_count - 1)
    wanted = jnp.where(row_slot < capacity, row_expert * capacity + row_slot, -1)
    token_hit = target[None, :] == wanted[:, None]
    table_source = jnp.where(
        (coded_index >= 0) & (coded_index < coded_rows), part_index * table_count + table_index, -1
    )
    table_hit = table_source[:, None] == jnp.arange(3 * table_count, dtype=jnp.int32)[None, :]
    placing = jnp.concatenate([token_hit, table_hit], axis=1).astype(jnp.bfloat16)
    buffer = jnp.dot(placing, sources, preferred_element_type=jnp.float32).astype(jnp.bfloat16)
    buffer = buffer.reshape(expert_count, span, feature_width)
    mine = lax.all_to_all(buffer, "expert", split_axis=0, concat_axis=2, tiled=True)[0]
    coded = mine[capacity : capacity + coded_rows].astype(jnp.float32)
    coded = coded.reshape(3, table_rows, mine.shape[1])
    tables = (coded[0] + coded[1]) + coded[2]
    mine = mine[:capacity]

    gains = tables[0]
    router_all = tables[1]
    picked = mine.astype(jnp.float32)
    d = picked.shape[1]
    scale = lax.rsqrt(jnp.sum(picked * picked, axis=1) / d + EPS)
    normed = (picked * scale[:, None] * gains[None, :]).astype(jnp.bfloat16)
    score = jax.nn.sigmoid(scale * jnp.sum(picked * gains[None, :] * router_all[None, :], axis=1))
    score_home = passed_along(score, SECTION, 1)

    block = lax.all_gather(normed, ("core", "chip"), axis=0, tiled=True)
    block, score_home, leaving = lax.optimization_barrier((block, score_home, activations))
    arrived = passed_along(leaving, SECTION, 1)
    block = block.reshape(n_core, n_chip * capacity, block.shape[1])
    core = lax.axis_index("core")

    def partial_rows(half):
        rows = lax.dynamic_index_in_dim(block, half, axis=0, keepdims=False)
        gate = feature_product(rows, gate_w[0])
        upper = feature_product(rows, up_w[0])
        hidden = (jax.nn.silu(gate) * upper).astype(jnp.bfloat16)
        hidden = hidden.reshape(n_chip, capacity, hidden.shape[1])
        doubled = jnp.concatenate([hidden, hidden], axis=0)
        hidden = lax.dynamic_slice_in_dim(doubled, n_chip - half, n_chip, axis=0)
        hidden = hidden.reshape(n_chip * capacity, hidden.shape[2])
        return jnp.dot(hidden, down_w[0], preferred_element_type=jnp.float32)

    give = partial_rows(core)
    give = lax.optimization_barrier(give.astype(jnp.bfloat16)).astype(jnp.float32).astype(jnp.bfloat16)
    taken = lax.ppermute(give, "core", [(0, 1), (1, 0)])
    keep = partial_rows(1 - core)
    keep = lax.optimization_barrier(keep.astype(jnp.bfloat16)).astype(jnp.float32).astype(jnp.bfloat16)
    pair = (keep.astype(jnp.float32) + taken.astype(jnp.float32)).astype(jnp.bfloat16)
    summed = lax.psum_scatter(pair, "chip", scatter_dimension=0, tiled=True)
    update_rows = (score_home[:, None] * summed.astype(jnp.float32)).astype(jnp.bfloat16)
    outgoing = update_rows.reshape(capacity, n_exp_dev, local_width).transpose(1, 0, 2)
    back = lax.all_to_all(outgoing, "expert", split_axis=0, concat_axis=0, tiled=True)
    flat_back = back.reshape(expert_count * capacity, local_width)

    picks = selected[0]
    token_count = arrived.shape[0]
    source = jnp.full((token_count,), -1, jnp.int32).at[picks].set(position)
    spread = (
        source[:, None] == jnp.arange(expert_count * capacity, dtype=jnp.int32)[None, :]
    ).astype(jnp.bfloat16)
    update = jnp.dot(spread, flat_back, preferred_element_type=jnp.float32)
    return (arrived.astype(jnp.float32) + update).astype(jnp.bfloat16)


def solution(mesh):
    n_section, n_expert = mesh.devices.shape
    split = jax.sharding.Mesh(
        mesh.devices.reshape(n_section // 2, 2, n_expert), ("chip", "core", "expert")
    )
    placed = (
        P(SECTION, "expert"),
        P(SECTION),
        P(SECTION, None),
        P(SECTION, None),
        P(None, "expert"),
        P("expert"),
        P("expert", SECTION, None),
        P("expert", SECTION, None),
        P("expert", SECTION, None),
    )
    return jax.shard_map(
        body, mesh=split, in_specs=placed, out_specs=P(SECTION, "expert"), check_vma=False
    )
```

```python
import jax
import jax.numpy as jnp
from jax import lax
from jax.sharding import PartitionSpec as P


EPS = 1e-05


SECTION = ("chip", "core")


def passed_along(block, axis, distance):
    names = axis if isinstance(axis, tuple) else (axis,)
    count = 1
    for name in names:
        count *= lax.axis_size(name)
    route = [((i - distance) % count, i) for i in range(count)]
    return lax.ppermute(block, axis, route)


def feature_product(block, weight):
    return lax.dot_general(
        block, weight, (((1,), (1,)), ((), ())), preferred_element_type=jnp.float32
    )


def body(activations, modality, selected, routes, norm_gain, router, gate_w, up_w, down_w):
    n_chip = lax.axis_size("chip")
    n_core = lax.axis_size("core")
    n_section = n_chip * n_core
    sel_count = selected.shape[1]
    expert_count = lax.axis_size("expert") * gate_w.shape[0]
    capacity = max(2, 3 * sel_count // (2 * expert_count))
    groups = n_section

    sel_next = passed_along(selected, SECTION, -1)[0]
    routes_next = passed_along(routes, SECTION, -1)[:, 0]
    rows = activations[sel_next]
    both = jnp.stack([routes_next, routes[:, 0]], axis=1)
    onehot = (both[:, :, None] == jnp.arange(expert_count, dtype=jnp.int32)[None, None, :]).astype(
        jnp.int32
    )
    slots = jnp.sum((jnp.cumsum(onehot, axis=0) - 1) * onehot, axis=2)
    targets = both * capacity + slots
    target = targets[:, 0]
    position = targets[:, 1]
    feature_width = rows.shape[1]
    n_exp_dev = lax.axis_size("expert")
    local_width = router.shape[0]
    tables = jnp.concatenate([norm_gain, router[None, :]], axis=0)
    table_count = tables.shape[0]
    parts = []
    rest = tables
    for _ in range(3):
        piece = rest.astype(jnp.bfloat16)
        parts.append(piece)
        rest = rest - piece.astype(jnp.float32)
    sources = jnp.concatenate([rows] + parts, axis=0)
    table_rows = 2
    coded_rows = 3 * table_rows
    span = capacity + -(-coded_rows // 8) * 8
    slot_of_row = jnp.arange(expert_count * span, dtype=jnp.int32)
    row_expert = slot_of_row // span
    row_slot = slot_of_row % span
    row_kind = (row_expert >= expert_count // 2).astype(jnp.int32)
    coded_index = row_slot - capacity
    part_index = coded_index // table_rows
    table_index = jnp.where(coded_index % table_rows == 0, row_kind, table_count - 1)
    wanted = jnp.where(row_slot < capacity, row_expert * capacity + row_slot, -1)
    token_hit = target[None, :] == wanted[:, None]
    table_source = jnp.where(
        (coded_index >= 0) & (coded_index < coded_rows), part_index * table_count + table_index, -1
    )
    table_hit = table_source[:, None] == jnp.arange(3 * table_count, dtype=jnp.int32)[None, :]
    placing = jnp.concatenate([token_hit, table_hit], axis=1).astype(jnp.bfloat16)
    buffer = jnp.dot(placing, sources, preferred_element_type=jnp.float32).astype(jnp.bfloat16)
    buffer = buffer.reshape(expert_count, span, feature_width)
    mine = lax.all_to_all(buffer, "expert", split_axis=0, concat_axis=2, tiled=True)[0]
    coded = mine[capacity : capacity + coded_rows].astype(jnp.float32)
    coded = coded.reshape(3, table_rows, mine.shape[1])
    tables = (coded[0] + coded[1]) + coded[2]
    mine = mine[:capacity]

    gains = tables[0]
    router_all = tables[1]
    picked = mine.astype(jnp.float32)
    d = picked.shape[1]
    scale = lax.rsqrt(jnp.sum(picked * picked, axis=1) / d + EPS)
    normed = (picked * scale[:, None] * gains[None, :]).astype(jnp.bfloat16)
    score = jax.nn.sigmoid(scale * jnp.sum(picked * gains[None, :] * router_all[None, :], axis=1))
    score_home = passed_along(score, SECTION, 1)

    block = lax.all_gather(normed, SECTION, axis=0, tiled=True)
    stacked = jnp.concatenate([gate_w[0], up_w[0]], axis=0)
    block, score_home, leaving, stacked = lax.optimization_barrier(
        (block, score_home, activations, stacked)
    )
    arrived = passed_along(leaving, SECTION, 1)
    both_products = feature_product(block, stacked)
    hidden_units = gate_w.shape[1]
    gate = both_products[:, :hidden_units]
    upper = both_products[:, hidden_units:]
    hidden = (jax.nn.silu(gate) * upper).astype(jnp.bfloat16)
    hidden_width = hidden.shape[1]
    order = []
    for core in range(n_core):
        for chip in range(n_chip):
            order.append((chip * n_core + core - 1) % n_section)
    hidden = jnp.take(
        hidden.reshape(groups, capacity, hidden_width), jnp.array(order, jnp.int32), axis=0
    ).reshape(groups * capacity, hidden_width)
    hidden = hidden.reshape(n_core, n_chip * capacity, hidden_width)
    core = lax.axis_index("core")

    def down_part(rows):
        part = jnp.dot(rows, down_w[0], preferred_element_type=jnp.float32)
        return lax.optimization_barrier(part.astype(jnp.bfloat16)).astype(jnp.float32).astype(jnp.bfloat16)

    give = down_part(lax.dynamic_index_in_dim(hidden, 1 - core, axis=0, keepdims=False))
    taken = lax.ppermute(give, "core", [(0, 1), (1, 0)])
    keep = down_part(lax.dynamic_index_in_dim(hidden, core, axis=0, keepdims=False))
    pair = (keep.astype(jnp.float32) + taken.astype(jnp.float32)).astype(jnp.bfloat16)
    summed = lax.psum_scatter(pair, "chip", scatter_dimension=0, tiled=True)
    update_rows = (score_home[:, None] * summed.astype(jnp.float32)).astype(jnp.bfloat16)
    outgoing = update_rows.reshape(capacity, n_exp_dev, local_width).transpose(1, 0, 2)
    back = lax.all_to_all(outgoing, "expert", split_axis=0, concat_axis=0, tiled=True)
    flat_back = back.reshape(expert_count * capacity, local_width)

    picks = selected[0]
    token_count = arrived.shape[0]
    source = jnp.full((token_count,), -1, jnp.int32).at[picks].set(position)
    spread = (
        source[:, None] == jnp.arange(expert_count * capacity, dtype=jnp.int32)[None, :]
    ).astype(jnp.bfloat16)
    update = jnp.dot(spread, flat_back, preferred_element_type=jnp.float32)
    return (arrived.astype(jnp.float32) + update).astype(jnp.bfloat16)


def solution(mesh):
    n_section, n_expert = mesh.devices.shape
    split = jax.sharding.Mesh(
        mesh.devices.reshape(n_section // 2, 2, n_expert), ("chip", "core", "expert")
    )
    placed = (
        P(SECTION, "expert"),
        P(SECTION),
        P(SECTION, None),
        P(SECTION, None),
        P(None, "expert"),
        P("expert"),
        P("expert", SECTION, None),
        P("expert", SECTION, None),
        P("expert", SECTION, None),
    )
    return jax.shard_map(
        body, mesh=split, in_specs=placed, out_specs=P(SECTION, "expert"), check_vma=False
    )
```

```python
import jax
import jax.numpy as jnp
from jax import lax
from jax.sharding import PartitionSpec as P


EPS = 1e-05


SECTION = ("chip", "core")


def passed_along(block, axis, distance):
    names = axis if isinstance(axis, tuple) else (axis,)
    count = 1
    for name in names:
        count *= lax.axis_size(name)
    route = [((i - distance) % count, i) for i in range(count)]
    return lax.ppermute(block, axis, route)


def feature_product(block, weight):
    return lax.dot_general(
        block, weight, (((1,), (1,)), ((), ())), preferred_element_type=jnp.float32
    )


def body(activations, modality, selected, routes, norm_gain, router, gate_w, up_w, down_w):
    n_chip = lax.axis_size("chip")
    n_core = lax.axis_size("core")
    n_section = n_chip * n_core
    sel_count = selected.shape[1]
    expert_count = lax.axis_size("expert") * gate_w.shape[0]
    capacity = max(2, 3 * sel_count // (2 * expert_count))
    groups = n_section

    sel_next = passed_along(selected, SECTION, -1)[0]
    routes_next = passed_along(routes, SECTION, -1)[:, 0]
    rows = activations[sel_next]
    both = jnp.stack([routes_next, routes[:, 0]], axis=1)
    onehot = (both[:, :, None] == jnp.arange(expert_count, dtype=jnp.int32)[None, None, :]).astype(
        jnp.int32
    )
    slots = jnp.sum((jnp.cumsum(onehot, axis=0) - 1) * onehot, axis=2)
    targets = both * capacity + slots
    target = targets[:, 0]
    position = targets[:, 1]
    feature_width = rows.shape[1]
    n_exp_dev = lax.axis_size("expert")
    local_width = router.shape[0]
    tables = jnp.concatenate([norm_gain, router[None, :]], axis=0)
    table_count = tables.shape[0]
    parts = []
    rest = tables
    for _ in range(3):
        piece = rest.astype(jnp.bfloat16)
        parts.append(piece)
        rest = rest - piece.astype(jnp.float32)
    sources = jnp.concatenate([rows] + parts, axis=0)
    table_rows = 2
    coded_rows = 3 * table_rows
    span = capacity + -(-coded_rows // 8) * 8
    slot_of_row = jnp.arange(expert_count * span, dtype=jnp.int32)
    row_expert = slot_of_row // span
    row_slot = slot_of_row % span
    row_kind = (row_expert >= expert_count // 2).astype(jnp.int32)
    coded_index = row_slot - capacity
    part_index = coded_index // table_rows
    table_index = jnp.where(coded_index % table_rows == 0, row_kind, table_count - 1)
    wanted = jnp.where(row_slot < capacity, row_expert * capacity + row_slot, -1)
    token_hit = target[None, :] == wanted[:, None]
    table_source = jnp.where(
        (coded_index >= 0) & (coded_index < coded_rows), part_index * table_count + table_index, -1
    )
    table_hit = table_source[:, None] == jnp.arange(3 * table_count, dtype=jnp.int32)[None, :]
    placing = jnp.concatenate([token_hit, table_hit], axis=1).astype(jnp.bfloat16)
    buffer = jnp.dot(placing, sources, preferred_element_type=jnp.float32).astype(jnp.bfloat16)
    buffer = buffer.reshape(expert_count, span, feature_width)
    mine = lax.all_to_all(buffer, "expert", split_axis=0, concat_axis=2, tiled=True)[0]
    coded = mine[capacity : capacity + coded_rows].astype(jnp.float32)
    coded = coded.reshape(3, table_rows, mine.shape[1])
    tables = (coded[0] + coded[1]) + coded[2]
    mine = mine[:capacity]

    gains = tables[0]
    router_all = tables[1]
    picked = mine.astype(jnp.float32)
    d = picked.shape[1]
    scale = lax.rsqrt(jnp.sum(picked * picked, axis=1) / d + EPS)
    normed = (picked * scale[:, None] * gains[None, :]).astype(jnp.bfloat16)
    score = jax.nn.sigmoid(scale * jnp.sum(picked * gains[None, :] * router_all[None, :], axis=1))
    score_home = passed_along(score, SECTION, 1)

    block = lax.all_gather(normed, SECTION, axis=0, tiled=True)
    block, score_home, leaving = lax.optimization_barrier((block, score_home, activations))
    arrived = passed_along(leaving, SECTION, 1)
    gate = feature_product(block, gate_w[0])
    upper = feature_product(block, up_w[0])
    hidden = (jax.nn.silu(gate) * upper).astype(jnp.bfloat16)
    hidden_width = hidden.shape[1]
    order = []
    for core in range(n_core):
        for chip in range(n_chip):
            order.append((chip * n_core + core - 1) % n_section)
    hidden = jnp.take(
        hidden.reshape(groups, capacity, hidden_width), jnp.array(order, jnp.int32), axis=0
    ).reshape(groups * capacity, hidden_width)
    hidden = hidden.reshape(n_core, n_chip * capacity, hidden_width)
    core = lax.axis_index("core")

    def down_part(rows):
        part = jnp.dot(rows, down_w[0], preferred_element_type=jnp.float32)
        return lax.optimization_barrier(part.astype(jnp.bfloat16)).astype(jnp.float32).astype(jnp.bfloat16)

    give = down_part(lax.dynamic_index_in_dim(hidden, 1 - core, axis=0, keepdims=False))
    taken = lax.ppermute(give, "core", [(0, 1), (1, 0)])
    keep = down_part(lax.dynamic_index_in_dim(hidden, core, axis=0, keepdims=False))
    pair = (keep.astype(jnp.float32) + taken.astype(jnp.float32)).astype(jnp.bfloat16)
    summed = lax.psum_scatter(pair, "chip", scatter_dimension=0, tiled=True)
    by_block = summed.reshape(capacity, n_exp_dev, local_width).transpose(1, 0, 2)
    outgoing = (score_home[None, :, None] * by_block.astype(jnp.float32)).astype(jnp.bfloat16)
    back = lax.all_to_all(outgoing, "expert", split_axis=0, concat_axis=0, tiled=True)
    flat_back = back.reshape(expert_count * capacity, local_width)

    picks = selected[0]
    token_count = arrived.shape[0]
    source = jnp.full((token_count,), -1, jnp.int32).at[picks].set(position)
    spread = (
        source[:, None] == jnp.arange(expert_count * capacity, dtype=jnp.int32)[None, :]
    ).astype(jnp.bfloat16)
    update = jnp.dot(spread, flat_back, preferred_element_type=jnp.float32)
    return (arrived.astype(jnp.float32) + update).astype(jnp.bfloat16)


def solution(mesh):
    n_section, n_expert = mesh.devices.shape
    split = jax.sharding.Mesh(
        mesh.devices.reshape(n_section // 2, 2, n_expert), ("chip", "core", "expert")
    )
    placed = (
        P(SECTION, "expert"),
        P(SECTION),
        P(SECTION, None),
        P(SECTION, None),
        P(None, "expert"),
        P("expert"),
        P("expert", SECTION, None),
        P("expert", SECTION, None),
        P("expert", SECTION, None),
    )
    return jax.shard_map(
        body, mesh=split, in_specs=placed, out_specs=P(SECTION, "expert"), check_vma=False
    )
```

```python
import jax
import jax.numpy as jnp
from jax import lax
from jax.sharding import PartitionSpec as P


EPS = 1e-05


SECTION = ("chip", "core")


def passed_along(block, axis, distance):
    names = axis if isinstance(axis, tuple) else (axis,)
    count = 1
    for name in names:
        count *= lax.axis_size(name)
    route = [((i - distance) % count, i) for i in range(count)]
    return lax.ppermute(block, axis, route)


def feature_product(block, weight):
    return lax.dot_general(
        block, weight, (((1,), (1,)), ((), ())), preferred_element_type=jnp.float32
    )


def body(activations, modality, selected, routes, norm_gain, router, gate_w, up_w, down_w):
    n_chip = lax.axis_size("chip")
    n_core = lax.axis_size("core")
    n_section = n_chip * n_core
    sel_count = selected.shape[1]
    expert_count = lax.axis_size("expert") * gate_w.shape[0]
    capacity = max(2, 3 * sel_count // (2 * expert_count))
    groups = n_section

    lists_next = passed_along(jnp.concatenate([selected, routes.T], axis=0), SECTION, -1)
    sel_next = lists_next[0]
    routes_next = lists_next[1]
    rows = activations[sel_next]
    both = jnp.stack([routes_next, routes[:, 0]], axis=1)
    onehot = (both[:, :, None] == jnp.arange(expert_count, dtype=jnp.int32)[None, None, :]).astype(
        jnp.int32
    )
    slots = jnp.sum((jnp.cumsum(onehot, axis=0) - 1) * onehot, axis=2)
    targets = both * capacity + slots
    target = targets[:, 0]
    position = targets[:, 1]
    feature_width = rows.shape[1]
    n_exp_dev = lax.axis_size("expert")
    local_width = router.shape[0]
    tables = jnp.concatenate([norm_gain, router[None, :]], axis=0)
    table_count = tables.shape[0]
    parts = []
    rest = tables
    for _ in range(3):
        piece = rest.astype(jnp.bfloat16)
        parts.append(piece)
        rest = rest - piece.astype(jnp.float32)
    sources = jnp.concatenate([rows] + parts, axis=0)
    table_rows = 2
    coded_rows = 3 * table_rows
    span = capacity + -(-coded_rows // 8) * 8
    slot_of_row = jnp.arange(expert_count * span, dtype=jnp.int32)
    row_expert = slot_of_row // span
    row_slot = slot_of_row % span
    row_kind = (row_expert >= expert_count // 2).astype(jnp.int32)
    coded_index = row_slot - capacity
    part_index = coded_index // table_rows
    table_index = jnp.where(coded_index % table_rows == 0, row_kind, table_count - 1)
    wanted = jnp.where(row_slot < capacity, row_expert * capacity + row_slot, -1)
    token_hit = target[None, :] == wanted[:, None]
    table_source = jnp.where(
        (coded_index >= 0) & (coded_index < coded_rows), part_index * table_count + table_index, -1
    )
    table_hit = table_source[:, None] == jnp.arange(3 * table_count, dtype=jnp.int32)[None, :]
    placing = jnp.concatenate([token_hit, table_hit], axis=1).astype(jnp.bfloat16)
    buffer = jnp.dot(placing, sources, preferred_element_type=jnp.float32).astype(jnp.bfloat16)
    buffer = buffer.reshape(expert_count, span, feature_width)
    mine = lax.all_to_all(buffer, "expert", split_axis=0, concat_axis=2, tiled=True)[0]
    coded = mine[capacity : capacity + coded_rows].astype(jnp.float32)
    coded = coded.reshape(3, table_rows, mine.shape[1])
    tables = (coded[0] + coded[1]) + coded[2]
    mine = mine[:capacity]

    gains = tables[0]
    router_all = tables[1]
    picked = mine.astype(jnp.float32)
    d = picked.shape[1]
    scale = lax.rsqrt(jnp.sum(picked * picked, axis=1) / d + EPS)
    normed = (picked * scale[:, None] * gains[None, :]).astype(jnp.bfloat16)
    score = jax.nn.sigmoid(scale * jnp.sum(picked * gains[None, :] * router_all[None, :], axis=1))
    score_home = passed_along(score, SECTION, 1)

    block = lax.all_gather(normed, SECTION, axis=0, tiled=True)
    stacked = jnp.concatenate([gate_w[0], up_w[0]], axis=0)
    block, score_home, leaving, stacked = lax.optimization_barrier(
        (block, score_home, activations, stacked)
    )
    arrived = passed_along(leaving, SECTION, 1)
    both_products = feature_product(block, stacked)
    hidden_units = gate_w.shape[1]
    gate = both_products[:, :hidden_units]
    upper = both_products[:, hidden_units:]
    hidden = (jax.nn.silu(gate) * upper).astype(jnp.bfloat16)
    hidden_width = hidden.shape[1]
    order = []
    for core in range(n_core):
        for chip in range(n_chip):
            order.append((chip * n_core + core - 1) % n_section)
    hidden = jnp.take(
        hidden.reshape(groups, capacity, hidden_width), jnp.array(order, jnp.int32), axis=0
    ).reshape(groups * capacity, hidden_width)
    hidden = hidden.reshape(n_core, n_chip * capacity, hidden_width)
    core = lax.axis_index("core")

    def down_part(rows):
        part = jnp.dot(rows, down_w[0], preferred_element_type=jnp.float32)
        return lax.optimization_barrier(part.astype(jnp.bfloat16)).astype(jnp.float32).astype(jnp.bfloat16)

    give = down_part(lax.dynamic_index_in_dim(hidden, 1 - core, axis=0, keepdims=False))
    taken = lax.ppermute(give, "core", [(0, 1), (1, 0)])
    keep = down_part(lax.dynamic_index_in_dim(hidden, core, axis=0, keepdims=False))
    pair = (keep.astype(jnp.float32) + taken.astype(jnp.float32)).astype(jnp.bfloat16)
    summed = lax.psum_scatter(pair, "chip", scatter_dimension=0, tiled=True)
    update_rows = (score_home[:, None] * summed.astype(jnp.float32)).astype(jnp.bfloat16)
    outgoing = update_rows.reshape(capacity, n_exp_dev, local_width).transpose(1, 0, 2)
    back = lax.all_to_all(outgoing, "expert", split_axis=0, concat_axis=0, tiled=True)
    flat_back = back.reshape(expert_count * capacity, local_width)

    picks = selected[0]
    token_count = arrived.shape[0]
    source = jnp.full((token_count,), -1, jnp.int32).at[picks].set(position)
    spread = (
        source[:, None] == jnp.arange(expert_count * capacity, dtype=jnp.int32)[None, :]
    ).astype(jnp.bfloat16)
    update = jnp.dot(spread, flat_back, preferred_element_type=jnp.float32)
    return (arrived.astype(jnp.float32) + update).astype(jnp.bfloat16)


def solution(mesh):
    n_section, n_expert = mesh.devices.shape
    split = jax.sharding.Mesh(
        mesh.devices.reshape(n_section // 2, 2, n_expert), ("chip", "core", "expert")
    )
    placed = (
        P(SECTION, "expert"),
        P(SECTION),
        P(SECTION, None),
        P(SECTION, None),
        P(None, "expert"),
        P("expert"),
        P("expert", SECTION, None),
        P("expert", SECTION, None),
        P("expert", SECTION, None),
    )
    return jax.shard_map(
        body, mesh=split, in_specs=placed, out_specs=P(SECTION, "expert"), check_vma=False
    )
```

```python
import jax
import jax.numpy as jnp
from jax import lax
from jax.sharding import PartitionSpec as P


EPS = 1e-05


SECTION = ("chip", "core")


def passed_along(block, axis, distance):
    names = axis if isinstance(axis, tuple) else (axis,)
    count = 1
    for name in names:
        count *= lax.axis_size(name)
    route = [((i - distance) % count, i) for i in range(count)]
    return lax.ppermute(block, axis, route)


def feature_product(block, weight):
    return lax.dot_general(
        block, weight, (((1,), (1,)), ((), ())), preferred_element_type=jnp.float32
    )


def body(activations, modality, selected, routes, norm_gain, router, gate_w, up_w, down_w):
    n_chip = lax.axis_size("chip")
    n_core = lax.axis_size("core")
    n_section = n_chip * n_core
    sel_count = selected.shape[1]
    expert_count = lax.axis_size("expert") * gate_w.shape[0]
    capacity = max(2, 3 * sel_count // (2 * expert_count))
    groups = n_section

    sel_next = passed_along(selected, SECTION, -1)[0]
    routes_next = passed_along(routes, SECTION, -1)[:, 0]
    rows = activations[sel_next]
    both = jnp.stack([routes_next, routes[:, 0]], axis=1)
    onehot = (both[:, :, None] == jnp.arange(expert_count, dtype=jnp.int32)[None, None, :]).astype(
        jnp.int32
    )
    slots = jnp.sum((jnp.cumsum(onehot, axis=0) - 1) * onehot, axis=2)
    targets = both * capacity + slots
    target = targets[:, 0]
    position = targets[:, 1]
    feature_width = rows.shape[1]
    n_exp_dev = lax.axis_size("expert")
    local_width = router.shape[0]
    tables = jnp.concatenate([norm_gain, router[None, :]], axis=0)
    table_count = tables.shape[0]
    parts = []
    rest = tables
    for _ in range(3):
        piece = rest.astype(jnp.bfloat16)
        parts.append(piece)
        rest = rest - piece.astype(jnp.float32)
    sources = jnp.concatenate([rows] + parts, axis=0)
    table_rows = 2
    coded_rows = 3 * table_rows
    span = capacity + -(-coded_rows // 8) * 8
    slot_of_row = jnp.arange(expert_count * span, dtype=jnp.int32)
    row_expert = slot_of_row // span
    row_slot = slot_of_row % span
    row_kind = (row_expert >= expert_count // 2).astype(jnp.int32)
    coded_index = row_slot - capacity
    part_index = coded_index // table_rows
    table_index = jnp.where(coded_index % table_rows == 0, row_kind, table_count - 1)
    wanted = jnp.where(row_slot < capacity, row_expert * capacity + row_slot, -1)
    token_hit = target[None, :] == wanted[:, None]
    table_source = jnp.where(
        (coded_index >= 0) & (coded_index < coded_rows), part_index * table_count + table_index, -1
    )
    table_hit = table_source[:, None] == jnp.arange(3 * table_count, dtype=jnp.int32)[None, :]
    placing = jnp.concatenate([token_hit, table_hit], axis=1).astype(jnp.bfloat16)
    buffer = jnp.dot(placing, sources, preferred_element_type=jnp.float32).astype(jnp.bfloat16)
    buffer = buffer.reshape(expert_count, span, feature_width)
    mine = lax.all_to_all(buffer, "expert", split_axis=0, concat_axis=2, tiled=True)[0]
    coded = mine[capacity : capacity + coded_rows].astype(jnp.float32)
    coded = coded.reshape(3, table_rows, mine.shape[1])
    tables = (coded[0] + coded[1]) + coded[2]
    mine = mine[:capacity]

    gains = tables[0]
    router_all = tables[1]
    picked = mine.astype(jnp.float32)
    d = picked.shape[1]
    scale = lax.rsqrt(jnp.sum(picked * picked, axis=1) / d + EPS)
    normed = (picked * scale[:, None] * gains[None, :]).astype(jnp.bfloat16)
    score = jax.nn.sigmoid(scale * jnp.sum(picked * gains[None, :] * router_all[None, :], axis=1))
    score_home = passed_along(score, SECTION, 1)

    block = lax.all_gather(normed, SECTION, axis=0, tiled=True)
    stacked = jnp.concatenate([gate_w[0], up_w[0]], axis=0)
    block, score_home, leaving, stacked = lax.optimization_barrier(
        (block, score_home, activations, stacked)
    )
    arrived = passed_along(leaving, SECTION, 1)
    both_products = feature_product(block, stacked)
    hidden_units = gate_w.shape[1]
    gate = both_products[:, :hidden_units]
    upper = both_products[:, hidden_units:]
    hidden = (jax.nn.silu(gate) * upper).astype(jnp.bfloat16)
    hidden_width = hidden.shape[1]
    order = []
    for core in range(n_core):
        for chip in range(n_chip):
            order.append((chip * n_core + core - 1) % n_section)
    order = jnp.array(order, jnp.int32).reshape(n_core, n_chip)
    grouped = hidden.reshape(groups, capacity, hidden_width)
    core = lax.axis_index("core")

    def half_rows(which):
        picked_groups = lax.dynamic_index_in_dim(order, which, axis=0, keepdims=False)
        return jnp.take(grouped, picked_groups, axis=0).reshape(n_chip * capacity, hidden_width)

    def down_part(rows):
        part = jnp.dot(rows, down_w[0], preferred_element_type=jnp.float32)
        return lax.optimization_barrier(part.astype(jnp.bfloat16)).astype(jnp.float32).astype(jnp.bfloat16)

    give = down_part(half_rows(1 - core))
    taken = lax.ppermute(give, "core", [(0, 1), (1, 0)])
    keep = down_part(half_rows(core))
    pair = (keep.astype(jnp.float32) + taken.astype(jnp.float32)).astype(jnp.bfloat16)
    summed = lax.psum_scatter(pair, "chip", scatter_dimension=0, tiled=True)
    update_rows = (score_home[:, None] * summed.astype(jnp.float32)).astype(jnp.bfloat16)
    outgoing = update_rows.reshape(capacity, n_exp_dev, local_width).transpose(1, 0, 2)
    back = lax.all_to_all(outgoing, "expert", split_axis=0, concat_axis=0, tiled=True)
    flat_back = back.reshape(expert_count * capacity, local_width)

    picks = selected[0]
    token_count = arrived.shape[0]
    source = jnp.full((token_count,), -1, jnp.int32).at[picks].set(position)
    spread = (
        source[:, None] == jnp.arange(expert_count * capacity, dtype=jnp.int32)[None, :]
    ).astype(jnp.bfloat16)
    update = jnp.dot(spread, flat_back, preferred_element_type=jnp.float32)
    return (arrived.astype(jnp.float32) + update).astype(jnp.bfloat16)


def solution(mesh):
    n_section, n_expert = mesh.devices.shape
    split = jax.sharding.Mesh(
        mesh.devices.reshape(n_section // 2, 2, n_expert), ("chip", "core", "expert")
    )
    placed = (
        P(SECTION, "expert"),
        P(SECTION),
        P(SECTION, None),
        P(SECTION, None),
        P(None, "expert"),
        P("expert"),
        P("expert", SECTION, None),
        P("expert", SECTION, None),
        P("expert", SECTION, None),
    )
    return jax.shard_map(
        body, mesh=split, in_specs=placed, out_specs=P(SECTION, "expert"), check_vma=False
    )
```
